512 devices in a mesh: req: 64 (over z, y_lo, x), tp: 8 (over y_hi, core).
Axes of the slice: x: 4, y: 8 (y_hi: 4, y_lo: 2; y = y_hi * 2 + y_lo), z: 8, core: 2. Of those that a mesh axis runs over, the one named last changes fastest.
Arguments:
- queries: bfloat16 [8192, 4096], P('req', 'tp'), may hold values from -48 to 48
- suffix_kv: bfloat16 [8192, 2, 2048], P('req', None, 'tp'), may hold values from -6 to 6
- window_kv: bfloat16 [2, 4096, 2, 2048], P(None, 'req', None, 'tp'), may hold values from -6 to 6
- sink_kv: bfloat16 [2, 4, 2, 2048], P(None, None, None, 'tp'), may hold values from -16 to 16
- lengths: int32 [64], P('req'), may hold values from 1 to 128, 4096 in all
- group_ids: int32 [64], replicated, may hold values from 0 to 1
- hidden_in: bfloat16 [8192, 2048], P('req', 'tp'), may hold values from -6 to 6
- router: bfloat16 [2048, 8], P('tp'), may hold values from -0.125 to 0.125
- picks: int32 [8192, 2], P('req'), may hold values from 0 to 7, all different within a row
Outputs:
- mixed: bfloat16 [8192, 4096], P('req', 'tp')
The draws below stay inside these ranges and needn't reach their ends.
All inputs are finite; a program needn't handle non-finite values. No bound on the sum of `lengths` on one device may be relied on, other than what follows from the above.
Results may differ from the reference program's by a relative error of at most 0.0024.
Values may be sent and summed in bfloat16 or wider, within the bound.
No kernel may reach another device: no remote copies, remote signals or barrier semaphores. Data moves between devices by JAX's collectives and lax.ppermute only.
A program may use at most 64 MiB of HBM per device.

```python
import math
import jax
import jax.numpy as jnp
import numpy as np
from jax import lax

D = 2048
KV_HEADS = 16
HEAD_DIM = 128
EXPERTS = 8
PICKS = 2
SINKS = 4
WIN = 4096
GROUPS = 2
SUF_MAX = 128
ROWS = 8192
TOKENS = 4096
N_REQ = 64


def joint_suffix(key):
    base = jax.random.fold_in(key, 7177)
    key_k, key_v, key_q = jax.random.split(base, 3)
    kv_shape = (ROWS, KV_HEADS, HEAD_DIM)
    q_shape = (ROWS, KV_HEADS, PICKS, HEAD_DIM)
    key_rows = jnp.clip(jax.random.normal(key_k, kv_shape, jnp.float32), -6.0, 6.0)
    value_rows = jnp.clip(jax.random.normal(key_v, kv_shape, jnp.float32), -6.0, 6.0)
    query_rows = 3.0 * jnp.clip(jax.random.normal(key_q, q_shape, jnp.float32), -5.0, 5.0)
    return (query_rows, key_rows, value_rows)


def draw_queries(key, part):
    query_rows, key_rows, value_rows = joint_suffix(key)
    return query_rows.reshape(ROWS, KV_HEADS * PICKS * HEAD_DIM).astype(jnp.bfloat16)


def draw_suffix_kv(key, part):
    query_rows, key_rows, value_rows = joint_suffix(key)
    stacked = jnp.stack([key_rows, value_rows], axis=1)
    return stacked.reshape(ROWS, 2, KV_HEADS * HEAD_DIM).astype(jnp.bfloat16)


def touch_ends(drawn, key, smallest, high):
    longest = drawn.shape.index(max(drawn.shape))
    spots = []
    for shift in (0, 1):
        where = [jax.random.randint(jax.random.fold_in(key, axis), (), 0, length) for axis, length in enumerate(drawn.shape)]
        where[longest] = (where[longest] + shift) % drawn.shape[longest]
        spots.append(tuple(where))
    return drawn.at[spots[0]].set(smallest).at[spots[1]].set(high)


def block_scale(rng, extent, cuts, smallest, top_value):
    level = 1.0
    for dim, shards_of in cuts:
        steps = jax.random.uniform(jax.random.fold_in(jax.random.fold_in(rng, 6), dim), (shards_of,), jnp.float32, smallest / len(cuts), top_value / len(cuts))
        level = level * jnp.repeat(jnp.exp(steps), extent[dim] // shards_of).reshape((-1,) + (1,) * (len(extent) - 1 - dim))
    return level


def different_ones(key, rows, number_of, top, lift):
    sequence = jax.random.permutation(jax.random.fold_in(key, 1), number_of)
    favour = sequence
    for power in range(3):
        favour = favour * favour // number_of
    favour = favour * lift // number_of
    lots = jax.random.randint(jax.random.fold_in(key, 2), (rows, number_of), 0, 4096) + favour
    sure = jax.random.permutation(jax.random.fold_in(key, 3), rows)[jnp.arange(number_of) % rows]
    lots = jnp.where(jnp.arange(rows)[:, None] == sure[None, :], 1 << 14, lots)
    score = lots * number_of + jnp.arange(number_of)
    return lax.top_k(score.astype(jnp.int32), top)[1].astype(jnp.int32)


def length_profile(number_of, total, bound, slope):
    portions = [(1 << 20) // math.isqrt(rank ** slope) + 1 for rank in range(2, number_of + 1)]
    rest, holding = total - bound - (number_of - 1), [1] * (number_of - 1)
    while rest > 0:
        candidates = [i for i in range(number_of - 1) if holding[i] < bound]
        mass, left = sum([portions[i] for i in candidates]), rest
        for i in candidates:
            addition = min(bound - holding[i], max(1, left * portions[i] // mass), rest)
            holding[i] = holding[i] + addition
            rest = rest - addition
    return np.array([bound] + holding)


def uneven_parts(rng, number_of, total, bound, skew):
    if number_of == 2:
        one = jax.random.randint(rng, (), max(1, total - bound), min(bound, total - 1) + 1)
        return jnp.stack([one, total - one])
    sizes = jnp.asarray(length_profile(number_of, total, bound, skew), jnp.int32)
    twos = (number_of - 1) // 2
    donor, sink = sizes[1:1 + 2 * twos:2], sizes[2:2 + 2 * twos:2]
    slack = jnp.minimum(donor - 1, bound - sink)
    moved = jax.random.randint(jax.random.fold_in(rng, 1), (twos,), 0, 1 << 20) % (slack + 1)
    sizes = sizes.at[1:1 + 2 * twos:2].set(donor - moved).at[2:2 + 2 * twos:2].set(sink + moved)
    return sizes[jax.random.permutation(jax.random.fold_in(rng, 2), number_of)]


def gaussian(stream_key, extent, scale, reach, pieces=(), kind=jnp.bfloat16):
    gain = block_scale(stream_key, extent, pieces, -0.22, 0.18) if pieces else 1.0
    entries = jax.random.normal(stream_key, extent, jnp.float32) * scale * gain
    return jnp.minimum(jnp.maximum(entries, -reach), reach).astype(kind)


def setup_inputs(seed: int = 0) -> dict:
    key_list = jax.random.split(jax.random.key(seed), 10)
    return {
        "queries": draw_queries(jax.random.fold_in(key_list[9], 71), 0),
        "suffix_kv": draw_suffix_kv(jax.random.fold_in(key_list[9], 71), 0),
        "window_kv": gaussian(key_list[2], (GROUPS, WIN, 2, KV_HEADS * HEAD_DIM), 1.0, 6.0, ((1, 64), (3, 8))),
        "sink_kv": gaussian(key_list[3], (GROUPS, SINKS, 2, KV_HEADS * HEAD_DIM), 3.0, 16.0, ((3, 8),)),
        "lengths": uneven_parts(key_list[4], N_REQ, TOKENS, SUF_MAX, 2).astype(jnp.int32),
        "group_ids": touch_ends(jax.random.randint(key_list[5], (N_REQ,), 0, GROUPS), jax.random.fold_in(key_list[5], 1), 0, GROUPS - 1).astype(jnp.int32),
        "hidden_in": gaussian(key_list[6], (ROWS, D), 1.0, 6.0, ((0, 64), (1, 8))),
        "router": gaussian(key_list[7], (D, EXPERTS), D ** -0.5, 0.125, ((0, 8),)),
        "picks": different_ones(key_list[8], ROWS, EXPERTS, PICKS, 2048),
    }


def request_attention(query_heads, suffix_rows, window_rows, sink_rows, length):
    row_count = query_heads.shape[0]
    head_count = query_heads.shape[1]
    head_dim = query_heads.shape[3]
    kv_rows = jnp.concatenate([sink_rows, window_rows, suffix_rows], axis=0)
    key_rows = kv_rows[:, 0].reshape(-1, head_count, head_dim).astype(jnp.float32)
    value_rows = kv_rows[:, 1].reshape(-1, head_count, head_dim).astype(jnp.float32)
    sink_count = sink_rows.shape[0]
    window_count = window_rows.shape[0]
    positions = jnp.arange(row_count, dtype=jnp.int32)[:, None]
    key_index = jnp.arange(key_rows.shape[0], dtype=jnp.int32)[None, :]
    window_index = key_index - sink_count
    suffix_index = key_index - sink_count - window_count
    is_sink = key_index < sink_count
    is_window = (window_index >= 0) & (suffix_index < 0) & (window_index > positions)
    is_suffix = (suffix_index >= 0) & (suffix_index <= positions)
    visible = (is_sink | is_window | is_suffix)[:, None, None, :]
    scores = jnp.einsum('qhpd,khd->qhpk', query_heads.astype(jnp.float32), key_rows) * (1.0 / math.sqrt(head_dim))
    row_max = lax.optimization_barrier(jnp.max(jnp.where(visible, scores, -jnp.inf), axis=3, keepdims=True))
    exponentials = jnp.where(visible, jnp.exp(scores - row_max), 0.0)
    totals = lax.optimization_barrier(jnp.sum(exponentials, axis=3))
    rounded = lax.optimization_barrier(exponentials.astype(jnp.bfloat16))
    weights = rounded.astype(jnp.float32)
    attended = jnp.einsum('qhpk,khd->qhpd', weights, value_rows) / totals[..., None]
    is_live = jnp.arange(row_count, dtype=jnp.int32) < length
    return (attended, is_live)

def reference(queries, suffix_kv, window_kv, sink_kv, lengths, group_ids, hidden_in, router, picks):
    logits = jnp.dot(hidden_in, router, preferred_element_type=jnp.float32)
    experts = jnp.arange(EXPERTS, dtype=jnp.int32)
    chosen = lax.optimization_barrier(jnp.sum(jnp.where(picks[:, :, None] == experts[None, None, :], logits[:, None, :], 0.0), axis=2))
    gate_values = jax.nn.sigmoid(chosen - chosen[:, ::-1])
    query_all = queries.reshape(N_REQ, SUF_MAX, KV_HEADS, PICKS, HEAD_DIM)
    suffix_all = suffix_kv.reshape(N_REQ, SUF_MAX, 2, KV_HEADS * HEAD_DIM)
    gate_all = gate_values.reshape(N_REQ, SUF_MAX, PICKS)

    def one_request(inputs):
        query_heads, suffix_rows, gate_rows, length, my_group = inputs
        window_rows = lax.dynamic_index_in_dim(window_kv, my_group, 0, keepdims=False)
        sink_rows = lax.dynamic_index_in_dim(sink_kv, my_group, 0, keepdims=False)
        attended, is_live = request_attention(query_heads, suffix_rows, window_rows, sink_rows, length)
        mixed_rows = jnp.where(is_live[:, None, None, None], attended * gate_rows[:, None, :, None], 0.0)
        return mixed_rows.astype(jnp.bfloat16)
    mixed_all = lax.map(one_request, (query_all, suffix_all, gate_all, lengths, group_ids))
    return mixed_all.reshape(N_REQ * SUF_MAX, KV_HEADS * PICKS * HEAD_DIM)
```

```python
import functools
import math

import jax
import jax.numpy as jnp
from jax import lax
from jax.experimental import pallas as pl
from jax.experimental.pallas import tpu as pltpu
from jax.sharding import PartitionSpec as P

HEAD_DIM = 128
PICKS = 2
CHUNK = 512


def attention_kernel(
    group_ref, q_ref, wk_ref, wv_ref, xk_ref, xv_ref, gate_ref, out_ref, score_ref, *, extra_sinks
):
    rows = q_ref.shape[0]
    window_rows = wk_ref.shape[0]
    extra_rows = xk_ref.shape[0]
    scale = 1.0 / math.sqrt(HEAD_DIM)
    q = q_ref[...]
    q_stack = jnp.concatenate([q[:, :HEAD_DIM], q[:, HEAD_DIM:]], axis=0)
    stacked = q_stack.shape[0]
    query_pos = lax.broadcasted_iota(jnp.int32, (stacked, CHUNK), 0) % rows
    nt = (((1,), (1,)), ((), ()))

    def scores_of(keys):
        return lax.dot_general(q_stack, keys, nt, preferred_element_type=jnp.float32) * scale

    extra = scores_of(xk_ref[...])
    extra_pos = lax.broadcasted_iota(jnp.int32, (stacked, extra_rows), 0) % rows
    extra_key = lax.broadcasted_iota(jnp.int32, (stacked, extra_rows), 1)
    extra_visible = (extra_key <= extra_pos) | (
        (extra_key >= rows) & (extra_key < rows + extra_sinks)
    )
    extra = jnp.where(extra_visible, extra, -jnp.inf)
    top = jnp.max(extra, axis=1, keepdims=True)

    chunk_count = window_rows // CHUNK
    for c in range(chunk_count):
        s = scores_of(wk_ref[pl.ds(c * CHUNK, CHUNK), :])
        if c == 0:
            key_pos = lax.broadcasted_iota(jnp.int32, (stacked, CHUNK), 1)
            s = jnp.where(key_pos > query_pos, s, -jnp.inf)
        score_ref[:, pl.ds(c * CHUNK, CHUNK)] = s
        top = jnp.maximum(top, jnp.max(s, axis=1, keepdims=True))

    e = jnp.exp(extra - top)
    total = jnp.sum(e, axis=1, keepdims=True)
    acc = jnp.dot(e.astype(jnp.bfloat16), xv_ref[...], preferred_element_type=jnp.float32)
    for c in range(chunk_count):
        e = jnp.exp(score_ref[:, pl.ds(c * CHUNK, CHUNK)] - top)
        total = total + jnp.sum(e, axis=1, keepdims=True)
        acc = acc + jnp.dot(
            e.astype(jnp.bfloat16),
            wv_ref[pl.ds(c * CHUNK, CHUNK), :],
            preferred_element_type=jnp.float32,
        )
    attended = acc / total
    gate = gate_ref[...]
    out_ref[:, :HEAD_DIM] = (attended[:rows] * gate[:, 0:1]).astype(out_ref.dtype)
    out_ref[:, HEAD_DIM:] = (attended[rows:] * gate[:, 1:2]).astype(out_ref.dtype)


def attend(group, queries, window, extra, gate_live, head_count, extra_sinks):
    rows = queries.shape[0]
    window_rows = window.shape[0]
    extra_rows = extra.shape[0]
    kernel = functools.partial(attention_kernel, extra_sinks=extra_sinks)
    grid_spec = pltpu.PrefetchScalarGridSpec(
        num_scalar_prefetch=1,
        grid=(head_count,),
        in_specs=[
            pl.BlockSpec((rows, PICKS * HEAD_DIM), lambda h, g: (0, h)),
            pl.BlockSpec((window_rows, HEAD_DIM), lambda h, g: (0, g[0] * 2 * head_count + h)),
            pl.BlockSpec(
                (window_rows, HEAD_DIM), lambda h, g: (0, g[0] * 2 * head_count + head_count + h)
            ),
            pl.BlockSpec((extra_rows, HEAD_DIM), lambda h, g: (0, h)),
            pl.BlockSpec((extra_rows, HEAD_DIM), lambda h, g: (0, head_count + h)),
            pl.BlockSpec((rows, PICKS), lambda h, g: (0, 0)),
        ],
        out_specs=pl.BlockSpec((rows, PICKS * HEAD_DIM), lambda h, g: (0, h)),
        scratch_shapes=[pltpu.VMEM((PICKS * rows, window_rows), jnp.float32)],
    )
    return pl.pallas_call(
        kernel,
        grid_spec=grid_spec,
        out_shape=jax.ShapeDtypeStruct((rows, head_count * PICKS * HEAD_DIM), jnp.bfloat16),
    )(group, queries, window, window, extra, extra, gate_live)


def body(queries, suffix_kv, window_kv, sink_kv, lengths, group_ids, hidden_in, router, picks):
    row_count = queries.shape[0]
    head_count = suffix_kv.shape[2] // HEAD_DIM
    partial_value = jnp.dot(hidden_in, router, preferred_element_type=jnp.float32)
    logits = lax.psum(partial_value, "tp")
    experts = jnp.arange(logits.shape[1], dtype=jnp.int32)
    chosen = jnp.sum(
        jnp.where(picks[:, :, None] == experts[None, None, :], logits[:, None, :], 0.0), axis=2
    )
    gate_values = jax.nn.sigmoid(chosen - chosen[:, ::-1])
    my_group = group_ids[lax.axis_index("req")]
    length = lengths[0]
    is_live = jnp.arange(row_count, dtype=jnp.int32) < length
    gate_live = jnp.where(is_live[:, None], gate_values, 0.0)

    groups = window_kv.shape[0]
    local = jnp.transpose(window_kv, (1, 0, 2, 3))
    local = local.reshape(local.shape[0], groups * 2 * head_count * HEAD_DIM)
    window = lax.all_gather(local, "req", axis=0, tiled=True)

    sink_rows = lax.dynamic_index_in_dim(sink_kv, my_group, 0, keepdims=False)
    sink_count = sink_rows.shape[0]
    extra_rows = 2 * row_count
    width = 2 * head_count * HEAD_DIM
    extra = jnp.concatenate(
        [
            suffix_kv.reshape(row_count, width),
            sink_rows.reshape(sink_count, width),
            jnp.zeros((extra_rows - row_count - sink_count, width), suffix_kv.dtype),
        ],
        axis=0,
    )
    group = my_group.reshape(1).astype(jnp.int32)
    return attend(group, queries, window, extra, gate_live, head_count, sink_count)


def solution(mesh):
    return jax.shard_map(
        body,
        mesh=mesh,
        in_specs=(
            P("req", "tp"),
            P("req", None, "tp"),
            P(None, "req", None, "tp"),
            P(None, None, None, "tp"),
            P("req"),
            P(),
            P("req", "tp"),
            P("tp", None),
            P("req", None),
        ),
        out_specs=P("req", "tp"),
        check_vma=False,
    )
```

```python
import functools
import math

import jax
import jax.numpy as jnp
from jax import lax
from jax.experimental import pallas as pl
from jax.experimental.pallas import tpu as pltpu
from jax.sharding import PartitionSpec as P

HEAD_DIM = 128
PICKS = 2
CHUNK = 512


def attention_kernel(
    group_ref, q_ref, wk_ref, wv_ref, xk_ref, xv_ref, gate_ref, out_ref, score_ref, *, extra_sinks
):
    rows = q_ref.shape[0]
    window_rows = wk_ref.shape[0]
    extra_rows = xk_ref.shape[0]
    scale = 1.0 / math.sqrt(HEAD_DIM)
    q = q_ref[...]
    q_stack = jnp.concatenate([q[:, :HEAD_DIM], q[:, HEAD_DIM:]], axis=0)
    stacked = q_stack.shape[0]
    query_pos = lax.broadcasted_iota(jnp.int32, (stacked, CHUNK), 0) % rows
    nt = (((1,), (1,)), ((), ()))

    def scores_of(keys):
        return lax.dot_general(q_stack, keys, nt, preferred_element_type=jnp.float32) * scale

    extra = scores_of(xk_ref[...])
    extra_pos = lax.broadcasted_iota(jnp.int32, (stacked, extra_rows), 0) % rows
    extra_key = lax.broadcasted_iota(jnp.int32, (stacked, extra_rows), 1)
    extra_visible = (extra_key <= extra_pos) | (
        (extra_key >= rows) & (extra_key < rows + extra_sinks)
    )
    extra = jnp.where(extra_visible, extra, -jnp.inf)
    top = jnp.max(extra, axis=1, keepdims=True)

    chunk_count = window_rows // CHUNK
    for c in range(chunk_count):
        s = scores_of(wk_ref[pl.ds(c * CHUNK, CHUNK), :])
        if c == 0:
            key_pos = lax.broadcasted_iota(jnp.int32, (stacked, CHUNK), 1)
            s = jnp.where(key_pos > query_pos, s, -jnp.inf)
        score_ref[:, pl.ds(c * CHUNK, CHUNK)] = s
        top = jnp.maximum(top, jnp.max(s, axis=1, keepdims=True))

    e = jnp.exp(extra - top)
    total = jnp.sum(e, axis=1, keepdims=True)
    acc = jnp.dot(e.astype(jnp.bfloat16), xv_ref[...], preferred_element_type=jnp.float32)
    for c in range(chunk_count):
        e = jnp.exp(score_ref[:, pl.ds(c * CHUNK, CHUNK)] - top)
        total = total + jnp.sum(e, axis=1, keepdims=True)
        acc = acc + jnp.dot(
            e.astype(jnp.bfloat16),
            wv_ref[pl.ds(c * CHUNK, CHUNK), :],
            preferred_element_type=jnp.float32,
        )
    attended = acc / total
    gate = gate_ref[...]
    out_ref[:, :HEAD_DIM] = (attended[:rows] * gate[:, 0:1]).astype(out_ref.dtype)
    out_ref[:, HEAD_DIM:] = (attended[rows:] * gate[:, 1:2]).astype(out_ref.dtype)


def attend(group, queries, window, extra, gate_live, head_count, extra_sinks):
    rows = queries.shape[0]
    window_rows = window.shape[0]
    extra_rows = extra.shape[0]
    kernel = functools.partial(attention_kernel, extra_sinks=extra_sinks)
    grid_spec = pltpu.PrefetchScalarGridSpec(
        num_scalar_prefetch=1,
        grid=(head_count,),
        in_specs=[
            pl.BlockSpec((rows, PICKS * HEAD_DIM), lambda h, g: (0, h)),
            pl.BlockSpec((window_rows, HEAD_DIM), lambda h, g: (0, h)),
            pl.BlockSpec((window_rows, HEAD_DIM), lambda h, g: (0, head_count + h)),
            pl.BlockSpec((extra_rows, HEAD_DIM), lambda h, g: (0, h)),
            pl.BlockSpec((extra_rows, HEAD_DIM), lambda h, g: (0, head_count + h)),
            pl.BlockSpec((rows, PICKS), lambda h, g: (0, 0)),
        ],
        out_specs=pl.BlockSpec((rows, PICKS * HEAD_DIM), lambda h, g: (0, h)),
        scratch_shapes=[pltpu.VMEM((PICKS * rows, window_rows), jnp.float32)],
    )
    return pl.pallas_call(
        kernel,
        grid_spec=grid_spec,
        out_shape=jax.ShapeDtypeStruct((rows, head_count * PICKS * HEAD_DIM), jnp.bfloat16),
    )(group, queries, window, window, extra, extra, gate_live)


def body(queries, suffix_kv, window_kv, sink_kv, lengths, group_ids, hidden_in, router, picks):
    row_count = queries.shape[0]
    head_count = suffix_kv.shape[2] // HEAD_DIM
    partial_value = jnp.dot(hidden_in, router, preferred_element_type=jnp.float32)
    logits = lax.psum(partial_value, "tp")
    experts = jnp.arange(logits.shape[1], dtype=jnp.int32)
    chosen = jnp.sum(
        jnp.where(picks[:, :, None] == experts[None, None, :], logits[:, None, :], 0.0), axis=2
    )
    gate_values = jax.nn.sigmoid(chosen - chosen[:, ::-1])
    my_group = group_ids[lax.axis_index("req")]
    length = lengths[0]
    is_live = jnp.arange(row_count, dtype=jnp.int32) < length
    gate_live = jnp.where(is_live[:, None], gate_values, 0.0)

    req_count = group_ids.shape[0]
    width = 2 * head_count * HEAD_DIM
    local = window_kv.reshape(window_kv.shape[0], window_kv.shape[1], width)
    outgoing = jnp.where(
        (group_ids == 0)[:, None, None], local[0][None], local[1][None]
    )
    received = lax.all_to_all(outgoing, "req", split_axis=0, concat_axis=0, tiled=True)
    window = received.reshape(req_count * local.shape[1], width)

    sink_rows = lax.dynamic_index_in_dim(sink_kv, my_group, 0, keepdims=False)
    sink_count = sink_rows.shape[0]
    extra_rows = 2 * row_count
    extra = jnp.concatenate(
        [
            suffix_kv.reshape(row_count, width),
            sink_rows.reshape(sink_count, width),
            jnp.zeros((extra_rows - row_count - sink_count, width), suffix_kv.dtype),
        ],
        axis=0,
    )
    group = my_group.reshape(1).astype(jnp.int32)
    return attend(group, queries, window, extra, gate_live, head_count, sink_count)


def solution(mesh):
    return jax.shard_map(
        body,
        mesh=mesh,
        in_specs=(
            P("req", "tp"),
            P("req", None, "tp"),
            P(None, "req", None, "tp"),
            P(None, None, None, "tp"),
            P("req"),
            P(),
            P("req", "tp"),
            P("tp", None),
            P("req", None),
        ),
        out_specs=P("req", "tp"),
        check_vma=False,
    )
```

```python
import functools
import math

import jax
import jax.numpy as jnp
from jax import lax
from jax.experimental import pallas as pl
from jax.experimental.pallas import tpu as pltpu
from jax.sharding import PartitionSpec as P

HEAD_DIM = 128
PICKS = 2
CHUNK = 512


def attention_kernel(
    group_ref,
    q_ref,
    wk_ref,
    wv_ref,
    xk_ref,
    xv_ref,
    gate_ref,
    out_ref,
    score_ref,
    *,
    extra_sinks,
    per_device,
    plane_count,
):
    rows = q_ref.shape[0]
    window_rows = wk_ref.shape[0]
    extra_rows = xk_ref.shape[0]
    scale = 1.0 / math.sqrt(HEAD_DIM)
    q = q_ref[...]
    q_stack = jnp.concatenate([q[:, :HEAD_DIM], q[:, HEAD_DIM:]], axis=0)
    stacked = q_stack.shape[0]
    query_pos = lax.broadcasted_iota(jnp.int32, (stacked, CHUNK), 0) % rows
    nt = (((1,), (1,)), ((), ()))

    def scores_of(keys):
        return lax.dot_general(q_stack, keys, nt, preferred_element_type=jnp.float32) * scale

    extra = scores_of(xk_ref[...])
    extra_pos = lax.broadcasted_iota(jnp.int32, (stacked, extra_rows), 0) % rows
    extra_key = lax.broadcasted_iota(jnp.int32, (stacked, extra_rows), 1)
    extra_visible = (extra_key <= extra_pos) | (
        (extra_key >= rows) & (extra_key < rows + extra_sinks)
    )
    extra = jnp.where(extra_visible, extra, -jnp.inf)
    top = jnp.max(extra, axis=1, keepdims=True)

    chunk_count = window_rows // CHUNK
    for c in range(chunk_count):
        s = scores_of(wk_ref[pl.ds(c * CHUNK, CHUNK), :])
        if c * per_device < rows:
            key_row = lax.broadcasted_iota(jnp.int32, (stacked, CHUNK), 1)
            key_pos = (
                (key_row // per_device) * plane_count + c
            ) * per_device + key_row % per_device
            s = jnp.where(key_pos > query_pos, s, -jnp.inf)
        score_ref[:, pl.ds(c * CHUNK, CHUNK)] = s
        top = jnp.maximum(top, jnp.max(s, axis=1, keepdims=True))

    e = jnp.exp(extra - top)
    total = jnp.sum(e, axis=1, keepdims=True)
    acc = jnp.dot(e.astype(jnp.bfloat16), xv_ref[...], preferred_element_type=jnp.float32)
    for c in range(chunk_count):
        e = jnp.exp(score_ref[:, pl.ds(c * CHUNK, CHUNK)] - top)
        total = total + jnp.sum(e, axis=1, keepdims=True)
        acc = acc + jnp.dot(
            e.astype(jnp.bfloat16),
            wv_ref[pl.ds(c * CHUNK, CHUNK), :],
            preferred_element_type=jnp.float32,
        )
    attended = acc / total
    gate = gate_ref[...]
    out_ref[:, :HEAD_DIM] = (attended[:rows] * gate[:, 0:1]).astype(out_ref.dtype)
    out_ref[:, HEAD_DIM:] = (attended[rows:] * gate[:, 1:2]).astype(out_ref.dtype)


def attend(group, queries, window, extra, gate_live, head_count, extra_sinks, per_device, plane_count):
    rows = queries.shape[0]
    window_rows = window.shape[0]
    extra_rows = extra.shape[0]
    kernel = functools.partial(
        attention_kernel,
        extra_sinks=extra_sinks,
        per_device=per_device,
        plane_count=plane_count,
    )
    grid_spec = pltpu.PrefetchScalarGridSpec(
        num_scalar_prefetch=1,
        grid=(head_count,),
        in_specs=[
            pl.BlockSpec((rows, PICKS * HEAD_DIM), lambda h, g: (0, h)),
            pl.BlockSpec((window_rows, HEAD_DIM), lambda h, g: (0, h)),
            pl.BlockSpec((window_rows, HEAD_DIM), lambda h, g: (0, head_count + h)),
            pl.BlockSpec((extra_rows, HEAD_DIM), lambda h, g: (0, h)),
            pl.BlockSpec((extra_rows, HEAD_DIM), lambda h, g: (0, head_count + h)),
            pl.BlockSpec((rows, PICKS), lambda h, g: (0, 0)),
        ],
        out_specs=pl.BlockSpec((rows, PICKS * HEAD_DIM), lambda h, g: (0, h)),
        scratch_shapes=[pltpu.VMEM((PICKS * rows, window_rows), jnp.float32)],
    )
    return pl.pallas_call(
        kernel,
        grid_spec=grid_spec,
        out_shape=jax.ShapeDtypeStruct((rows, head_count * PICKS * HEAD_DIM), jnp.bfloat16),
    )(group, queries, window, window, extra, extra, gate_live)


def body(queries, suffix_kv, window_kv, sink_kv, lengths, group_ids, hidden_in, router, picks):
    row_count = queries.shape[0]
    head_count = suffix_kv.shape[2] // HEAD_DIM
    partial_value = jnp.dot(hidden_in, router, preferred_element_type=jnp.float32)
    logits = lax.psum(partial_value, "tp")
    experts = jnp.arange(logits.shape[1], dtype=jnp.int32)
    chosen = jnp.sum(
        jnp.where(picks[:, :, None] == experts[None, None, :], logits[:, None, :], 0.0), axis=2
    )
    gate_values = jax.nn.sigmoid(chosen - chosen[:, ::-1])
    z_count = lax.axis_size("z")
    plane_count = lax.axis_size("ylo") * lax.axis_size("x")
    z_me = lax.axis_index("z")
    plane_me = lax.axis_index("ylo") * lax.axis_size("x") + lax.axis_index("x")
    my_group = group_ids[z_me * plane_count + plane_me]
    length = lengths[0]
    is_live = jnp.arange(row_count, dtype=jnp.int32) < length
    gate_live = jnp.where(is_live[:, None], gate_values, 0.0)

    width = 2 * head_count * HEAD_DIM
    per_device = window_kv.shape[1]
    local = window_kv.reshape(window_kv.shape[0], per_device, width)
    arrived = [local]
    for shift in range(1, z_count):
        pairs = [(j, (j + shift) % z_count) for j in range(z_count)]
        arrived.append(lax.ppermute(local, "z", pairs))
    by_shift = jnp.stack(arrived)
    by_z = jnp.take(by_shift, (z_me - jnp.arange(z_count)) % z_count, axis=0)
    peer_groups = lax.dynamic_slice_in_dim(group_ids, z_me * plane_count, plane_count)
    outgoing = jnp.where(
        (peer_groups == 0)[:, None, None, None], by_z[None, :, 0], by_z[None, :, 1]
    )
    received = lax.all_to_all(outgoing, ("ylo", "x"), split_axis=0, concat_axis=0, tiled=True)
    window = received.reshape(plane_count * z_count * per_device, width)

    sink_rows = lax.dynamic_index_in_dim(sink_kv, my_group, 0, keepdims=False)
    sink_count = sink_rows.shape[0]
    extra_rows = 2 * row_count
    extra = jnp.concatenate(
        [
            suffix_kv.reshape(row_count, width),
            sink_rows.reshape(sink_count, width),
            jnp.zeros((extra_rows - row_count - sink_count, width), suffix_kv.dtype),
        ],
        axis=0,
    )
    group = my_group.reshape(1).astype(jnp.int32)
    return attend(
        group, queries, window, extra, gate_live, head_count, sink_count, per_device, plane_count
    )


def solution(mesh):
    plane_ylo, plane_x = 2, 4
    z_count = mesh.shape["req"] // (plane_ylo * plane_x)
    devices = mesh.devices.reshape(z_count, plane_ylo, plane_x, mesh.shape["tp"])
    inner = jax.sharding.Mesh(devices, ("z", "ylo", "x", "tp"))
    req = ("z", "ylo", "x")
    return jax.shard_map(
        body,
        mesh=inner,
        in_specs=(
            P(req, "tp"),
            P(req, None, "tp"),
            P(None, req, None, "tp"),
            P(None, None, None, "tp"),
            P(req),
            P(),
            P(req, "tp"),
            P("tp", None),
            P(req, None),
        ),
        out_specs=P(req, "tp"),
        check_vma=False,
    )
```

```python
import functools
import math

import jax
import jax.numpy as jnp
from jax import lax
from jax.experimental import pallas as pl
from jax.experimental.pallas import tpu as pltpu
from jax.sharding import PartitionSpec as P

HEAD_DIM = 128
PICKS = 2
CHUNK = 512


def attention_kernel(q_ref, pos_ref, *refs, extra_sinks, per_device, part_slots):
    part_count = len(part_slots)
    window_refs = refs[: 2 * part_count]
    xk_ref, xv_ref, gate_ref, out_ref, score_ref = refs[2 * part_count :]
    rows = q_ref.shape[0]
    scale = 1.0 / math.sqrt(HEAD_DIM)
    q = q_ref[...]
    q_stack = jnp.concatenate([q[:, :HEAD_DIM], q[:, HEAD_DIM:]], axis=0)
    stacked = q_stack.shape[0]
    query_pos = lax.broadcasted_iota(jnp.int32, (stacked, 1), 0) % rows
    nt = (((1,), (1,)), ((), ()))

    def scores_of(keys):
        return lax.dot_general(q_stack, keys, nt, preferred_element_type=jnp.float32) * scale

    extra_rows = xk_ref.shape[0]
    extra = scores_of(xk_ref[...])
    extra_pos = lax.broadcasted_iota(jnp.int32, (stacked, extra_rows), 0) % rows
    extra_key = lax.broadcasted_iota(jnp.int32, (stacked, extra_rows), 1)
    extra_visible = (extra_key <= extra_pos) | (
        (extra_key >= rows) & (extra_key < rows + extra_sinks)
    )
    extra = jnp.where(extra_visible, extra, -jnp.inf)
    top = jnp.max(extra, axis=1, keepdims=True)

    chunks = []
    offset = 0
    for part, slots in enumerate(part_slots):
        for c in range(window_refs[2 * part].shape[0] // CHUNK):
            chunks.append((part, c, offset))
            s = scores_of(window_refs[2 * part][pl.ds(c * CHUNK, CHUNK), :])
            if (c * CHUNK) // (slots * per_device) * per_device < rows:
                key_pos = pos_ref[:, pl.ds(offset, CHUNK)]
                s = jnp.where(key_pos > query_pos, s, -jnp.inf)
            score_ref[:, pl.ds(offset, CHUNK)] = s
            top = jnp.maximum(top, jnp.max(s, axis=1, keepdims=True))
            offset += CHUNK

    e = jnp.exp(extra - top)
    total = jnp.sum(e, axis=1, keepdims=True)
    acc = jnp.dot(e.astype(jnp.bfloat16), xv_ref[...], preferred_element_type=jnp.float32)
    for part, c, offset in chunks:
        e = jnp.exp(score_ref[:, pl.ds(offset, CHUNK)] - top)
        total = total + jnp.sum(e, axis=1, keepdims=True)
        acc = acc + jnp.dot(
            e.astype(jnp.bfloat16),
            window_refs[2 * part + 1][pl.ds(c * CHUNK, CHUNK), :],
            preferred_element_type=jnp.float32,
        )
    attended = acc / total
    gate = gate_ref[...]
    out_ref[:, :HEAD_DIM] = (attended[:rows] * gate[:, 0:1]).astype(out_ref.dtype)
    out_ref[:, HEAD_DIM:] = (attended[rows:] * gate[:, 1:2]).astype(out_ref.dtype)


def attend(queries, key_pos, parts, part_slots, extra, gate_live, head_count, extra_sinks, per_device):
    rows = queries.shape[0]
    extra_rows = extra.shape[0]
    window_rows = key_pos.shape[1]
    kernel = functools.partial(
        attention_kernel,
        extra_sinks=extra_sinks,
        per_device=per_device,
        part_slots=part_slots,
    )
    window_specs = []
    window_args = []
    for part in parts:
        window_specs.append(pl.BlockSpec((part.shape[0], HEAD_DIM), lambda h: (0, h)))
        window_specs.append(pl.BlockSpec((part.shape[0], HEAD_DIM), lambda h: (0, head_count + h)))
        window_args += [part, part]
    return pl.pallas_call(
        kernel,
        grid=(head_count,),
        in_specs=[
            pl.BlockSpec((rows, PICKS * HEAD_DIM), lambda h: (0, h)),
            pl.BlockSpec((1, window_rows), lambda h: (0, 0)),
        ]
        + window_specs
        + [
            pl.BlockSpec((extra_rows, HEAD_DIM), lambda h: (0, h)),
            pl.BlockSpec((extra_rows, HEAD_DIM), lambda h: (0, head_count + h)),
            pl.BlockSpec((rows, PICKS), lambda h: (0, 0)),
        ],
        out_specs=pl.BlockSpec((rows, PICKS * HEAD_DIM), lambda h: (0, h)),
        scratch_shapes=[pltpu.VMEM((PICKS * rows, window_rows), jnp.float32)],
        out_shape=jax.ShapeDtypeStruct((rows, head_count * PICKS * HEAD_DIM), jnp.bfloat16),
    )(queries, key_pos, *window_args, extra, extra, gate_live)


def body(queries, suffix_kv, window_kv, sink_kv, lengths, group_ids, hidden_in, router, picks):
    row_count = queries.shape[0]
    head_count = suffix_kv.shape[2] // HEAD_DIM
    partial_value = jnp.dot(hidden_in, router, preferred_element_type=jnp.float32)
    logits = lax.psum(partial_value, "tp")
    experts = jnp.arange(logits.shape[1], dtype=jnp.int32)
    chosen = jnp.sum(
        jnp.where(picks[:, :, None] == experts[None, None, :], logits[:, None, :], 0.0), axis=2
    )
    gate_values = jax.nn.sigmoid(chosen - chosen[:, ::-1])
    z_count = lax.axis_size("z")
    plane_count = lax.axis_size("ylo") * lax.axis_size("x")
    z_me = lax.axis_index("z")
    plane_me = lax.axis_index("ylo") * lax.axis_size("x") + lax.axis_index("x")
    my_group = group_ids[z_me * plane_count + plane_me]
    length = lengths[0]
    is_live = jnp.arange(row_count, dtype=jnp.int32) < length
    gate_live = jnp.where(is_live[:, None], gate_values, 0.0)

    width = 2 * head_count * HEAD_DIM
    per_device = window_kv.shape[1]
    local = window_kv.reshape(window_kv.shape[0], per_device, width)
    near = [0] + [k for k in range(1, z_count) if min(k, z_count - k) == 1]
    far = sorted(
        (k for k in range(1, z_count) if k not in near), key=lambda k: min(k, z_count - k)
    )
    part_shifts = (tuple(near), tuple(far))
    peer_groups = lax.dynamic_slice_in_dim(group_ids, z_me * plane_count, plane_count)
    parts = []
    positions = []
    for shifts in part_shifts:
        arrived = []
        for shift in shifts:
            if shift == 0:
                arrived.append(local)
            else:
                pairs = [(j, (j + shift) % z_count) for j in range(z_count)]
                arrived.append(lax.ppermute(local, "z", pairs))
        by_slot = jnp.stack(arrived)
        outgoing = jnp.where(
            (peer_groups == 0)[:, None, None, None], by_slot[None, :, 0], by_slot[None, :, 1]
        )
        received = lax.all_to_all(
            outgoing, ("ylo", "x"), split_axis=0, concat_axis=0, tiled=True
        )
        parts.append(received.reshape(plane_count * len(shifts) * per_device, width))
        z_of_slot = (z_me - jnp.array(shifts, jnp.int32)) % z_count
        plane_ids = jnp.arange(plane_count, dtype=jnp.int32)
        row_ids = jnp.arange(per_device, dtype=jnp.int32)
        part_pos = (
            (z_of_slot[None, :, None] * plane_count + plane_ids[:, None, None]) * per_device
            + row_ids[None, None, :]
        )
        positions.append(part_pos.reshape(-1))

    sink_rows = lax.dynamic_index_in_dim(sink_kv, my_group, 0, keepdims=False)
    sink_count = sink_rows.shape[0]
    extra_rows = 2 * row_count
    extra = jnp.concatenate(
        [
            suffix_kv.reshape(row_count, width),
            sink_rows.reshape(sink_count, width),
            jnp.zeros((extra_rows - row_count - sink_count, width), suffix_kv.dtype),
        ],
        axis=0,
    )
    key_pos = jnp.concatenate(positions).reshape(1, -1)
    part_slots = tuple(len(shifts) for shifts in part_shifts)
    return attend(
        queries, key_pos, parts, part_slots, extra, gate_live, head_count, sink_count, per_device
    )


def solution(mesh):
    plane_ylo, plane_x = 2, 4
    z_count = mesh.shape["req"] // (plane_ylo * plane_x)
    devices = mesh.devices.reshape(z_count, plane_ylo, plane_x, mesh.shape["tp"])
    inner = jax.sharding.Mesh(devices, ("z", "ylo", "x", "tp"))
    req = ("z", "ylo", "x")
    return jax.shard_map(
        body,
        mesh=inner,
        in_specs=(
            P(req, "tp"),
            P(req, None, "tp"),
            P(None, req, None, "tp"),
            P(None, None, None, "tp"),
            P(req),
            P(),
            P(req, "tp"),
            P("tp", None),
            P(req, None),
        ),
        out_specs=P(req, "tp"),
        check_vma=False,
    )
```

```python
import functools
import math

import jax
import jax.numpy as jnp
from jax import lax
from jax.experimental import pallas as pl
from jax.experimental.pallas import tpu as pltpu
from jax.sharding import PartitionSpec as P

HEAD_DIM = 128
PICKS = 2
CHUNK = 512


def attention_kernel(q_ref, pos_ref, *refs, extra_sinks, per_device, part_slots):
    part_count = len(part_slots)
    window_refs = refs[: 2 * part_count]
    xk_ref, xv_ref, gate_ref, out_ref, score_ref = refs[2 * part_count :]
    rows = q_ref.shape[0]
    scale = 1.0 / math.sqrt(HEAD_DIM)
    q = q_ref[...]
    q_stack = jnp.concatenate([q[:, :HEAD_DIM], q[:, HEAD_DIM:]], axis=0)
    stacked = q_stack.shape[0]
    query_pos = lax.broadcasted_iota(jnp.int32, (stacked, 1), 0) % rows
    nt = (((1,), (1,)), ((), ()))

    def scores_of(keys):
        return lax.dot_general(q_stack, keys, nt, preferred_element_type=jnp.float32) * scale

    extra_rows = xk_ref.shape[0]
    extra = scores_of(xk_ref[...])
    extra_pos = lax.broadcasted_iota(jnp.int32, (stacked, extra_rows), 0) % rows
    extra_key = lax.broadcasted_iota(jnp.int32, (stacked, extra_rows), 1)
    extra_visible = (extra_key <= extra_pos) | (
        (extra_key >= rows) & (extra_key < rows + extra_sinks)
    )
    extra = jnp.where(extra_visible, extra, -jnp.inf)
    top = jnp.max(extra, axis=1, keepdims=True)

    chunks = []
    offset = 0
    for part, slots in enumerate(part_slots):
        for c in range(window_refs[2 * part].shape[0] // CHUNK):
            chunks.append((part, c, offset))
            s = scores_of(window_refs[2 * part][pl.ds(c * CHUNK, CHUNK), :])
            if (c * CHUNK) // (slots * per_device) * per_device < rows:
                key_pos = pos_ref[:, pl.ds(offset, CHUNK)]
                s = jnp.where(key_pos > query_pos, s, -jnp.inf)
            score_ref[:, pl.ds(offset, CHUNK)] = s
            top = jnp.maximum(top, jnp.max(s, axis=1, keepdims=True))
            offset += CHUNK

    e = jnp.exp(extra - top)
    total = jnp.sum(e, axis=1, keepdims=True)
    acc = jnp.dot(e.astype(jnp.bfloat16), xv_ref[...], preferred_element_type=jnp.float32)
    for part, c, offset in chunks:
        e = jnp.exp(score_ref[:, pl.ds(offset, CHUNK)] - top)
        total = total + jnp.sum(e, axis=1, keepdims=True)
        acc = acc + jnp.dot(
            e.astype(jnp.bfloat16),
            window_refs[2 * part + 1][pl.ds(c * CHUNK, CHUNK), :],
            preferred_element_type=jnp.float32,
        )
    attended = acc / total
    gate = gate_ref[...]
    out_ref[:, :HEAD_DIM] = (attended[:rows] * gate[:, 0:1]).astype(out_ref.dtype)
    out_ref[:, HEAD_DIM:] = (attended[rows:] * gate[:, 1:2]).astype(out_ref.dtype)


def attend(queries, key_pos, parts, part_slots, extra, gate_live, head_count, extra_sinks, per_device):
    rows = queries.shape[0]
    extra_rows = extra.shape[0]
    window_rows = key_pos.shape[1]
    kernel = functools.partial(
        attention_kernel,
        extra_sinks=extra_sinks,
        per_device=per_device,
        part_slots=part_slots,
    )
    window_specs = []
    window_args = []
    for part in parts:
        window_specs.append(pl.BlockSpec((part.shape[0], HEAD_DIM), lambda h: (0, h)))
        window_specs.append(pl.BlockSpec((part.shape[0], HEAD_DIM), lambda h: (0, head_count + h)))
        window_args += [part, part]
    return pl.pallas_call(
        kernel,
        grid=(head_count,),
        in_specs=[
            pl.BlockSpec((rows, PICKS * HEAD_DIM), lambda h: (0, h)),
            pl.BlockSpec((1, window_rows), lambda h: (0, 0)),
        ]
        + window_specs
        + [
            pl.BlockSpec((extra_rows, HEAD_DIM), lambda h: (0, h)),
            pl.BlockSpec((extra_rows, HEAD_DIM), lambda h: (0, head_count + h)),
            pl.BlockSpec((rows, PICKS), lambda h: (0, 0)),
        ],
        out_specs=pl.BlockSpec((rows, PICKS * HEAD_DIM), lambda h: (0, h)),
        scratch_shapes=[pltpu.VMEM((PICKS * rows, window_rows), jnp.float32)],
        out_shape=jax.ShapeDtypeStruct((rows, head_count * PICKS * HEAD_DIM), jnp.bfloat16),
    )(queries, key_pos, *window_args, extra, extra, gate_live)


def body(queries, suffix_kv, window_kv, sink_kv, lengths, group_ids, hidden_in, router, picks):
    row_count = queries.shape[0]
    head_count = suffix_kv.shape[2] // HEAD_DIM
    partial_value = jnp.dot(hidden_in, router, preferred_element_type=jnp.float32)
    logits = lax.psum(partial_value, "tp")
    experts = jnp.arange(logits.shape[1], dtype=jnp.int32)
    chosen = jnp.sum(
        jnp.where(picks[:, :, None] == experts[None, None, :], logits[:, None, :], 0.0), axis=2
    )
    gate_values = jax.nn.sigmoid(chosen - chosen[:, ::-1])
    z_count = lax.axis_size("z")
    plane_count = lax.axis_size("ylo") * lax.axis_size("x")
    z_me = lax.axis_index("z")
    plane_me = lax.axis_index("ylo") * lax.axis_size("x") + lax.axis_index("x")
    my_group = group_ids[z_me * plane_count + plane_me]
    length = lengths[0]
    is_live = jnp.arange(row_count, dtype=jnp.int32) < length
    gate_live = jnp.where(is_live[:, None], gate_values, 0.0)

    width = 2 * head_count * HEAD_DIM
    per_device = window_kv.shape[1]
    local = window_kv.reshape(window_kv.shape[0], per_device, width)
    def shifted(value, shift):
        pairs = [(j, (j + shift) % z_count) for j in range(z_count)]
        return lax.ppermute(value, "z", pairs)

    up = shifted(local, 1)
    down = shifted(local, z_count - 1)
    near_shifts = (0, 1, z_count - 1)
    near_slots = [local, up, down]
    far_up = shifted(jnp.stack([down, local, up]), 3)
    far_down = shifted(jnp.stack([local, up]), z_count - 3)
    far_shifts = (2, 3, 4, z_count - 3, z_count - 2)
    far_slots = [far_up[0], far_up[1], far_up[2], far_down[0], far_down[1]]
    part_shifts = (near_shifts, far_shifts)
    peer_groups = lax.dynamic_slice_in_dim(group_ids, z_me * plane_count, plane_count)
    parts = []
    positions = []
    for shifts, arrived in zip(part_shifts, (near_slots, far_slots)):
        by_slot = jnp.stack(arrived)
        outgoing = jnp.where(
            (peer_groups == 0)[:, None, None, None], by_slot[None, :, 0], by_slot[None, :, 1]
        )
        received = lax.all_to_all(
            outgoing, ("ylo", "x"), split_axis=0, concat_axis=0, tiled=True
        )
        parts.append(received.reshape(plane_count * len(shifts) * per_device, width))
        z_of_slot = (z_me - jnp.array(shifts, jnp.int32)) % z_count
        plane_ids = jnp.arange(plane_count, dtype=jnp.int32)
        row_ids = jnp.arange(per_device, dtype=jnp.int32)
        part_pos = (
            (z_of_slot[None, :, None] * plane_count + plane_ids[:, None, None]) * per_device
            + row_ids[None, None, :]
        )
        positions.append(part_pos.reshape(-1))

    sink_rows = lax.dynamic_index_in_dim(sink_kv, my_group, 0, keepdims=False)
    sink_count = sink_rows.shape[0]
    extra_rows = 2 * row_count
    extra = jnp.concatenate(
        [
            suffix_kv.reshape(row_count, width),
            sink_rows.reshape(sink_count, width),
            jnp.zeros((extra_rows - row_count - sink_count, width), suffix_kv.dtype),
        ],
        axis=0,
    )
    key_pos = jnp.concatenate(positions).reshape(1, -1)
    part_slots = tuple(len(shifts) for shifts in part_shifts)
    return attend(
        queries, key_pos, parts, part_slots, extra, gate_live, head_count, sink_count, per_device
    )


def solution(mesh):
    plane_ylo, plane_x = 2, 4
    z_count = mesh.shape["req"] // (plane_ylo * plane_x)
    devices = mesh.devices.reshape(z_count, plane_ylo, plane_x, mesh.shape["tp"])
    inner = jax.sharding.Mesh(devices, ("z", "ylo", "x", "tp"))
    req = ("z", "ylo", "x")
    return jax.shard_map(
        body,
        mesh=inner,
        in_specs=(
            P(req, "tp"),
            P(req, None, "tp"),
            P(None, req, None, "tp"),
            P(None, None, None, "tp"),
            P(req),
            P(),
            P(req, "tp"),
            P("tp", None),
            P(req, None),
        ),
        out_specs=P(req, "tp"),
        check_vma=False,
    )
```

```python
import functools
import math

import jax
import jax.numpy as jnp
from jax import lax
from jax.experimental import pallas as pl
from jax.experimental.pallas import tpu as pltpu
from jax.sharding import PartitionSpec as P

HEAD_DIM = 128
PICKS = 2
CHUNK = 512


def attention_kernel(q_ref, pos_ref, *refs, extra_sinks, per_device, plane_rows):
    part_count = len(plane_rows)
    window_refs = refs[: 2 * part_count]
    xk_ref, xv_ref, gate_ref, out_ref, score_ref = refs[2 * part_count :]
    rows = q_ref.shape[0]
    scale = 1.0 / math.sqrt(HEAD_DIM)
    q = q_ref[...]
    q_stack = jnp.concatenate([q[:, :HEAD_DIM], q[:, HEAD_DIM:]], axis=0)
    stacked = q_stack.shape[0]
    query_pos = lax.broadcasted_iota(jnp.int32, (stacked, 1), 0) % rows
    nt = (((1,), (1,)), ((), ()))

    def scores_of(keys):
        return lax.dot_general(q_stack, keys, nt, preferred_element_type=jnp.float32) * scale

    extra_rows = xk_ref.shape[0]
    extra = scores_of(xk_ref[...])
    extra_pos = lax.broadcasted_iota(jnp.int32, (stacked, extra_rows), 0) % rows
    extra_key = lax.broadcasted_iota(jnp.int32, (stacked, extra_rows), 1)
    extra_visible = (extra_key <= extra_pos) | (
        (extra_key >= rows) & (extra_key < rows + extra_sinks)
    )
    extra = jnp.where(extra_visible, extra, -jnp.inf)
    top = jnp.max(extra, axis=1, keepdims=True)

    chunks = []
    offset = 0
    for part, stride in enumerate(plane_rows):
        for c in range(window_refs[2 * part].shape[0] // CHUNK):
            chunks.append((part, c, offset))
            s = scores_of(window_refs[2 * part][pl.ds(c * CHUNK, CHUNK), :])
            if (c * CHUNK) // stride * per_device < rows:
                key_pos = pos_ref[:, pl.ds(offset, CHUNK)]
                s = jnp.where(key_pos > query_pos, s, -jnp.inf)
            score_ref[:, pl.ds(offset, CHUNK)] = s
            top = jnp.maximum(top, jnp.max(s, axis=1, keepdims=True))
            offset += CHUNK

    e = jnp.exp(extra - top)
    total = jnp.sum(e, axis=1, keepdims=True)
    acc = jnp.dot(e.astype(jnp.bfloat16), xv_ref[...], preferred_element_type=jnp.float32)
    for part, c, offset in chunks:
        e = jnp.exp(score_ref[:, pl.ds(offset, CHUNK)] - top)
        total = total + jnp.sum(e, axis=1, keepdims=True)
        acc = acc + jnp.dot(
            e.astype(jnp.bfloat16),
            window_refs[2 * part + 1][pl.ds(c * CHUNK, CHUNK), :],
            preferred_element_type=jnp.float32,
        )
    attended = acc / total
    gate = gate_ref[...]
    out_ref[:, :HEAD_DIM] = (attended[:rows] * gate[:, 0:1]).astype(out_ref.dtype)
    out_ref[:, HEAD_DIM:] = (attended[rows:] * gate[:, 1:2]).astype(out_ref.dtype)


def attend(queries, key_pos, parts, plane_rows, extra, gate_live, head_count, extra_sinks, per_device):
    rows = queries.shape[0]
    extra_rows = extra.shape[0]
    window_rows = key_pos.shape[1]
    kernel = functools.partial(
        attention_kernel,
        extra_sinks=extra_sinks,
        per_device=per_device,
        plane_rows=plane_rows,
    )
    window_specs = []
    window_args = []
    for part in parts:
        window_specs.append(pl.BlockSpec((part.shape[0], HEAD_DIM), lambda h: (0, h)))
        window_specs.append(pl.BlockSpec((part.shape[0], HEAD_DIM), lambda h: (0, head_count + h)))
        window_args += [part, part]
    return pl.pallas_call(
        kernel,
        grid=(head_count,),
        in_specs=[
            pl.BlockSpec((rows, PICKS * HEAD_DIM), lambda h: (0, h)),
            pl.BlockSpec((1, window_rows), lambda h: (0, 0)),
        ]
        + window_specs
        + [
            pl.BlockSpec((extra_rows, HEAD_DIM), lambda h: (0, h)),
            pl.BlockSpec((extra_rows, HEAD_DIM), lambda h: (0, head_count + h)),
            pl.BlockSpec((rows, PICKS), lambda h: (0, 0)),
        ],
        out_specs=pl.BlockSpec((rows, PICKS * HEAD_DIM), lambda h: (0, h)),
        scratch_shapes=[pltpu.VMEM((PICKS * rows, window_rows), jnp.float32)],
        out_shape=jax.ShapeDtypeStruct((rows, head_count * PICKS * HEAD_DIM), jnp.bfloat16),
    )(queries, key_pos, *window_args, extra, extra, gate_live)


def body(queries, suffix_kv, window_kv, sink_kv, lengths, group_ids, hidden_in, router, picks):
    row_count = queries.shape[0]
    head_count = suffix_kv.shape[2] // HEAD_DIM
    partial_value = jnp.dot(hidden_in, router, preferred_element_type=jnp.float32)
    logits = lax.psum(partial_value, "tp")
    experts = jnp.arange(logits.shape[1], dtype=jnp.int32)
    chosen = jnp.sum(
        jnp.where(picks[:, :, None] == experts[None, None, :], logits[:, None, :], 0.0), axis=2
    )
    gate_values = jax.nn.sigmoid(chosen - chosen[:, ::-1])
    z_count = lax.axis_size("z")
    plane_count = lax.axis_size("ylo") * lax.axis_size("x")
    z_me = lax.axis_index("z")
    plane_me = lax.axis_index("ylo") * lax.axis_size("x") + lax.axis_index("x")
    my_group = group_ids[z_me * plane_count + plane_me]
    length = lengths[0]
    is_live = jnp.arange(row_count, dtype=jnp.int32) < length
    gate_live = jnp.where(is_live[:, None], gate_values, 0.0)

    width = 2 * head_count * HEAD_DIM
    per_device = window_kv.shape[1]
    local = window_kv.reshape(window_kv.shape[0], per_device, width)
    def shifted(value, shift):
        pairs = [(j, (j + shift) % z_count) for j in range(z_count)]
        return lax.ppermute(value, "z", pairs)

    half = per_device // 2
    up = shifted(local, 1)
    down = shifted(local, z_count - 1)
    far_up = shifted(jnp.concatenate([down, local, up[:, :half]], axis=1), 3)
    far_down = shifted(jnp.concatenate([local, up, down[:, half:]], axis=1), z_count - 3)
    near_pieces = ((0, 0, per_device), (1, 0, per_device), (z_count - 1, 0, per_device))
    far_pieces = (
        (2, 0, per_device),
        (3, 0, per_device),
        (4, 0, half),
        (z_count - 3, 0, per_device),
        (z_count - 2, 0, per_device),
        (4, half, per_device - half),
    )
    part_pieces = (near_pieces, far_pieces)
    part_data = (jnp.concatenate([local, up, down], axis=1), jnp.concatenate([far_up, far_down], axis=1))
    peer_groups = lax.dynamic_slice_in_dim(group_ids, z_me * plane_count, plane_count)
    plane_ids = jnp.arange(plane_count, dtype=jnp.int32)
    parts = []
    positions = []
    for pieces, data in zip(part_pieces, part_data):
        outgoing = jnp.where((peer_groups == 0)[:, None, None], data[None, 0], data[None, 1])
        received = lax.all_to_all(
            outgoing, ("ylo", "x"), split_axis=0, concat_axis=0, tiled=True
        )
        parts.append(received.reshape(plane_count * data.shape[1], width))
        piece_pos = []
        for shift, first, count in pieces:
            z_of = (z_me - shift) % z_count
            rows_of = first + jnp.arange(count, dtype=jnp.int32)
            piece_pos.append(
                (z_of * plane_count + plane_ids[:, None]) * per_device + rows_of[None, :]
            )
        positions.append(jnp.concatenate(piece_pos, axis=1).reshape(-1))

    sink_rows = lax.dynamic_index_in_dim(sink_kv, my_group, 0, keepdims=False)
    sink_count = sink_rows.shape[0]
    extra_rows = 2 * row_count
    extra = jnp.concatenate(
        [
            suffix_kv.reshape(row_count, width),
            sink_rows.reshape(sink_count, width),
            jnp.zeros((extra_rows - row_count - sink_count, width), suffix_kv.dtype),
        ],
        axis=0,
    )
    key_pos = jnp.concatenate(positions).reshape(1, -1)
    plane_rows = tuple(data.shape[1] for data in part_data)
    return attend(
        queries, key_pos, parts, plane_rows, extra, gate_live, head_count, sink_count, per_device
    )


def solution(mesh):
    plane_ylo, plane_x = 2, 4
    z_count = mesh.shape["req"] // (plane_ylo * plane_x)
    devices = mesh.devices.reshape(z_count, plane_ylo, plane_x, mesh.shape["tp"])
    inner = jax.sharding.Mesh(devices, ("z", "ylo", "x", "tp"))
    req = ("z", "ylo", "x")
    return jax.shard_map(
        body,
        mesh=inner,
        in_specs=(
            P(req, "tp"),
            P(req, None, "tp"),
            P(None, req, None, "tp"),
            P(None, None, None, "tp"),
            P(req),
            P(),
            P(req, "tp"),
            P("tp", None),
            P(req, None),
        ),
        out_specs=P(req, "tp"),
        check_vma=False,
    )
```

```python
import functools
import math

import jax
import jax.numpy as jnp
from jax import lax
from jax.experimental import pallas as pl
from jax.experimental.pallas import tpu as pltpu
from jax.sharding import PartitionSpec as P

HEAD_DIM = 128
PICKS = 2
CHUNK = 512


def attention_kernel(q_ref, pos_ref, *refs, extra_sinks, per_device, plane_rows):
    part_count = len(plane_rows)
    window_refs = refs[: 2 * part_count]
    xk_ref, xv_ref, gate_ref, out_ref, score_ref = refs[2 * part_count :]
    rows = q_ref.shape[0]
    scale = 1.0 / math.sqrt(HEAD_DIM)
    q = q_ref[...]
    q_stack = jnp.concatenate([q[:, :HEAD_DIM], q[:, HEAD_DIM:]], axis=0)
    stacked = q_stack.shape[0]
    query_pos = lax.broadcasted_iota(jnp.int32, (stacked, 1), 0) % rows
    nt = (((1,), (1,)), ((), ()))

    def scores_of(keys):
        return lax.dot_general(q_stack, keys, nt, preferred_element_type=jnp.float32) * scale

    extra_rows = xk_ref.shape[0]
    extra = scores_of(xk_ref[...])
    extra_pos = lax.broadcasted_iota(jnp.int32, (stacked, extra_rows), 0) % rows
    extra_key = lax.broadcasted_iota(jnp.int32, (stacked, extra_rows), 1)
    extra_visible = (extra_key <= extra_pos) | (
        (extra_key >= rows) & (extra_key < rows + extra_sinks)
    )
    extra = jnp.where(extra_visible, extra, -jnp.inf)
    top = jnp.max(extra, axis=1, keepdims=True)

    chunks = []
    offset = 0
    for part, stride in enumerate(plane_rows):
        for c in range(window_refs[2 * part].shape[0] // CHUNK):
            chunks.append((part, c, offset))
            s = scores_of(window_refs[2 * part][pl.ds(c * CHUNK, CHUNK), :])
            if (c * CHUNK) // stride * per_device < rows:
                key_pos = pos_ref[:, pl.ds(offset, CHUNK)]
                s = jnp.where(key_pos > query_pos, s, -jnp.inf)
            score_ref[:, pl.ds(offset, CHUNK)] = s
            top = jnp.maximum(top, jnp.max(s, axis=1, keepdims=True))
            offset += CHUNK

    e = jnp.exp(extra - top)
    total = jnp.sum(e, axis=1, keepdims=True)
    acc = jnp.dot(e.astype(jnp.bfloat16), xv_ref[...], preferred_element_type=jnp.float32)
    for part, c, offset in chunks:
        e = jnp.exp(score_ref[:, pl.ds(offset, CHUNK)] - top)
        total = total + jnp.sum(e, axis=1, keepdims=True)
        acc = acc + jnp.dot(
            e.astype(jnp.bfloat16),
            window_refs[2 * part + 1][pl.ds(c * CHUNK, CHUNK), :],
            preferred_element_type=jnp.float32,
        )
    attended = acc / total
    gate = gate_ref[...]
    out_ref[:, :HEAD_DIM] = (attended[:rows] * gate[:, 0:1]).astype(out_ref.dtype)
    out_ref[:, HEAD_DIM:] = (attended[rows:] * gate[:, 1:2]).astype(out_ref.dtype)


def attend(queries, key_pos, parts, plane_rows, extra, gate_live, head_count, extra_sinks, per_device):
    rows = queries.shape[0]
    extra_rows = extra.shape[0]
    window_rows = key_pos.shape[1]
    kernel = functools.partial(
        attention_kernel,
        extra_sinks=extra_sinks,
        per_device=per_device,
        plane_rows=plane_rows,
    )
    window_specs = []
    window_args = []
    for part in parts:
        window_specs.append(pl.BlockSpec((part.shape[0], HEAD_DIM), lambda h: (0, h)))
        window_specs.append(pl.BlockSpec((part.shape[0], HEAD_DIM), lambda h: (0, head_count + h)))
        window_args += [part, part]
    return pl.pallas_call(
        kernel,
        grid=(head_count,),
        in_specs=[
            pl.BlockSpec((rows, PICKS * HEAD_DIM), lambda h: (0, h)),
            pl.BlockSpec((1, window_rows), lambda h: (0, 0)),
        ]
        + window_specs
        + [
            pl.BlockSpec((extra_rows, HEAD_DIM), lambda h: (0, h)),
            pl.BlockSpec((extra_rows, HEAD_DIM), lambda h: (0, head_count + h)),
            pl.BlockSpec((rows, PICKS), lambda h: (0, 0)),
        ],
        out_specs=pl.BlockSpec((rows, PICKS * HEAD_DIM), lambda h: (0, h)),
        scratch_shapes=[pltpu.VMEM((PICKS * rows, window_rows), jnp.float32)],
        out_shape=jax.ShapeDtypeStruct((rows, head_count * PICKS * HEAD_DIM), jnp.bfloat16),
    )(queries, key_pos, *window_args, extra, extra, gate_live)


def body(queries, suffix_kv, window_kv, sink_kv, lengths, group_ids, hidden_in, router, picks):
    row_count = queries.shape[0]
    head_count = suffix_kv.shape[2] // HEAD_DIM
    partial_value = jnp.dot(hidden_in, router, preferred_element_type=jnp.float32)
    logits = lax.psum(partial_value, "tp")
    experts = jnp.arange(logits.shape[1], dtype=jnp.int32)
    chosen = jnp.sum(
        jnp.where(picks[:, :, None] == experts[None, None, :], logits[:, None, :], 0.0), axis=2
    )
    gate_values = jax.nn.sigmoid(chosen - chosen[:, ::-1])
    z_count = lax.axis_size("z")
    plane_count = lax.axis_size("ylo") * lax.axis_size("x")
    z_me = lax.axis_index("z")
    plane_me = lax.axis_index("ylo") * lax.axis_size("x") + lax.axis_index("x")
    my_group = group_ids[z_me * plane_count + plane_me]
    length = lengths[0]
    is_live = jnp.arange(row_count, dtype=jnp.int32) < length
    gate_live = jnp.where(is_live[:, None], gate_values, 0.0)

    width = 2 * head_count * HEAD_DIM
    per_device = window_kv.shape[1]
    local = window_kv.reshape(window_kv.shape[0], per_device, width)
    local, logits = lax.optimization_barrier((local, logits))
    def shifted(value, shift):
        pairs = [(j, (j + shift) % z_count) for j in range(z_count)]
        return lax.ppermute(value, "z", pairs)

    half = per_device // 2
    up = shifted(local, 1)
    down = shifted(local, z_count - 1)
    far_up = shifted(jnp.concatenate([down, local, up[:, :half]], axis=1), 3)
    far_down = shifted(jnp.concatenate([local, up, down[:, half:]], axis=1), z_count - 3)
    near_pieces = ((0, 0, per_device), (1, 0, per_device), (z_count - 1, 0, per_device))
    far_pieces = (
        (2, 0, per_device),
        (3, 0, per_device),
        (4, 0, half),
        (z_count - 3, 0, per_device),
        (z_count - 2, 0, per_device),
        (4, half, per_device - half),
    )
    part_pieces = (near_pieces, far_pieces)
    part_data = (jnp.concatenate([local, up, down], axis=1), jnp.concatenate([far_up, far_down], axis=1))
    peer_groups = lax.dynamic_slice_in_dim(group_ids, z_me * plane_count, plane_count)
    plane_ids = jnp.arange(plane_count, dtype=jnp.int32)
    parts = []
    positions = []
    for pieces, data in zip(part_pieces, part_data):
        outgoing = jnp.where((peer_groups == 0)[:, None, None], data[None, 0], data[None, 1])
        received = lax.all_to_all(
            outgoing, ("ylo", "x"), split_axis=0, concat_axis=0, tiled=True
        )
        parts.append(received.reshape(plane_count * data.shape[1], width))
        piece_pos = []
        for shift, first, count in pieces:
            z_of = (z_me - shift) % z_count
            rows_of = first + jnp.arange(count, dtype=jnp.int32)
            piece_pos.append(
                (z_of * plane_count + plane_ids[:, None]) * per_device + rows_of[None, :]
            )
        positions.append(jnp.concatenate(piece_pos, axis=1).reshape(-1))

    sink_rows = lax.dynamic_index_in_dim(sink_kv, my_group, 0, keepdims=False)
    sink_count = sink_rows.shape[0]
    extra_rows = 2 * row_count
    extra = jnp.concatenate(
        [
            suffix_kv.reshape(row_count, width),
            sink_rows.reshape(sink_count, width),
            jnp.zeros((extra_rows - row_count - sink_count, width), suffix_kv.dtype),
        ],
        axis=0,
    )
    key_pos = jnp.concatenate(positions).reshape(1, -1)
    plane_rows = tuple(data.shape[1] for data in part_data)
    return attend(
        queries, key_pos, parts, plane_rows, extra, gate_live, head_count, sink_count, per_device
    )


def solution(mesh):
    plane_ylo, plane_x = 2, 4
    z_count = mesh.shape["req"] // (plane_ylo * plane_x)
    devices = mesh.devices.reshape(z_count, plane_ylo, plane_x, mesh.shape["tp"])
    inner = jax.sharding.Mesh(devices, ("z", "ylo", "x", "tp"))
    req = ("z", "ylo", "x")
    return jax.shard_map(
        body,
        mesh=inner,
        in_specs=(
            P(req, "tp"),
            P(req, None, "tp"),
            P(None, req, None, "tp"),
            P(None, None, None, "tp"),
            P(req),
            P(),
            P(req, "tp"),
            P("tp", None),
            P(req, None),
        ),
        out_specs=P(req, "tp"),
        check_vma=False,
    )
```

```python
import functools
import math

import jax
import jax.numpy as jnp
from jax import lax
from jax.experimental import pallas as pl
from jax.experimental.pallas import tpu as pltpu
from jax.sharding import PartitionSpec as P

HEAD_DIM = 128
PICKS = 2
CHUNK = 512


def stacked_queries(q_ref):
    q = q_ref[...]
    return jnp.concatenate([q[:, :HEAD_DIM], q[:, HEAD_DIM:]], axis=0)


def window_scores(q_stack, pos_ref, wk_ref, score_ref, rows, per_device, stride, scale):
    stacked = q_stack.shape[0]
    query_pos = lax.broadcasted_iota(jnp.int32, (stacked, 1), 0) % rows
    nt = (((1,), (1,)), ((), ()))
    top = jnp.full((stacked, 1), -jnp.inf, jnp.float32)
    for c in range(wk_ref.shape[0] // CHUNK):
        keys = wk_ref[pl.ds(c * CHUNK, CHUNK), :]
        s = lax.dot_general(q_stack, keys, nt, preferred_element_type=jnp.float32) * scale
        if (c * CHUNK) // stride * per_device < rows:
            key_pos = pos_ref[:, pl.ds(c * CHUNK, CHUNK)]
            s = jnp.where(key_pos > query_pos, s, -jnp.inf)
        score_ref[:, pl.ds(c * CHUNK, CHUNK)] = s
        top = jnp.maximum(top, jnp.max(s, axis=1, keepdims=True))
    return top


def window_sums(wv_ref, score_ref, top, total, acc):
    for c in range(wv_ref.shape[0] // CHUNK):
        e = jnp.exp(score_ref[:, pl.ds(c * CHUNK, CHUNK)] - top)
        total = total + jnp.sum(e, axis=1, keepdims=True)
        acc = acc + jnp.dot(
            e.astype(jnp.bfloat16),
            wv_ref[pl.ds(c * CHUNK, CHUNK), :],
            preferred_element_type=jnp.float32,
        )
    return total, acc


def first_kernel(
    q_ref,
    pos_ref,
    wk_ref,
    wv_ref,
    xk_ref,
    xv_ref,
    acc_ref,
    top_ref,
    total_ref,
    score_ref,
    *,
    extra_sinks,
    per_device,
    stride,
):
    rows = q_ref.shape[0]
    scale = 1.0 / math.sqrt(HEAD_DIM)
    q_stack = stacked_queries(q_ref)
    stacked = q_stack.shape[0]
    nt = (((1,), (1,)), ((), ()))
    extra_rows = xk_ref.shape[0]
    extra = (
        lax.dot_general(q_stack, xk_ref[...], nt, preferred_element_type=jnp.float32) * scale
    )
    extra_pos = lax.broadcasted_iota(jnp.int32, (stacked, extra_rows), 0) % rows
    extra_key = lax.broadcasted_iota(jnp.int32, (stacked, extra_rows), 1)
    extra_visible = (extra_key <= extra_pos) | (
        (extra_key >= rows) & (extra_key < rows + extra_sinks)
    )
    extra = jnp.where(extra_visible, extra, -jnp.inf)
    top = jnp.maximum(
        jnp.max(extra, axis=1, keepdims=True),
        window_scores(q_stack, pos_ref, wk_ref, score_ref, rows, per_device, stride, scale),
    )
    e = jnp.exp(extra - top)
    total = jnp.sum(e, axis=1, keepdims=True)
    acc = jnp.dot(e.astype(jnp.bfloat16), xv_ref[...], preferred_element_type=jnp.float32)
    total, acc = window_sums(wv_ref, score_ref, top, total, acc)
    acc_ref[...] = acc
    top_ref[...] = jnp.broadcast_to(top, top_ref.shape)
    total_ref[...] = jnp.broadcast_to(total, total_ref.shape)


def second_kernel(
    q_ref,
    pos_ref,
    wk_ref,
    wv_ref,
    acc_ref,
    top_ref,
    total_ref,
    gate_ref,
    out_ref,
    score_ref,
    *,
    per_device,
    stride,
):
    rows = q_ref.shape[0]
    scale = 1.0 / math.sqrt(HEAD_DIM)
    q_stack = stacked_queries(q_ref)
    first_top = top_ref[:, 0:1]
    top = jnp.maximum(
        first_top,
        window_scores(q_stack, pos_ref, wk_ref, score_ref, rows, per_device, stride, scale),
    )
    factor = jnp.exp(first_top - top)
    total, acc = window_sums(
        wv_ref, score_ref, top, total_ref[:, 0:1] * factor, acc_ref[...] * factor
    )
    attended = acc / total
    gate = gate_ref[...]
    out_ref[:, :HEAD_DIM] = (attended[:rows] * gate[:, 0:1]).astype(out_ref.dtype)
    out_ref[:, HEAD_DIM:] = (attended[rows:] * gate[:, 1:2]).astype(out_ref.dtype)


def attend(queries, key_pos, parts, plane_rows, extra, gate_live, head_count, extra_sinks, per_device):
    rows = queries.shape[0]
    stacked = PICKS * rows
    extra_rows = extra.shape[0]
    first, second = parts
    first_rows = first.shape[0]
    second_rows = second.shape[0]
    first_pos = key_pos[:, :first_rows]
    second_pos = key_pos[:, first_rows:]
    q_spec = pl.BlockSpec((rows, PICKS * HEAD_DIM), lambda h: (0, h))
    state_spec = pl.BlockSpec((None, stacked, HEAD_DIM), lambda h: (h, 0, 0))
    state_shape = jax.ShapeDtypeStruct((head_count, stacked, HEAD_DIM), jnp.float32)

    def key_spec(part_rows):
        return pl.BlockSpec((part_rows, HEAD_DIM), lambda h: (0, h))

    def value_spec(part_rows):
        return pl.BlockSpec((part_rows, HEAD_DIM), lambda h: (0, head_count + h))

    acc, top, total = pl.pallas_call(
        functools.partial(
            first_kernel, extra_sinks=extra_sinks, per_device=per_device, stride=plane_rows[0]
        ),
        grid=(head_count,),
        in_specs=[
            q_spec,
            pl.BlockSpec((1, first_rows), lambda h: (0, 0)),
            key_spec(first_rows),
            value_spec(first_rows),
            key_spec(extra_rows),
            value_spec(extra_rows),
        ],
        out_specs=[state_spec, state_spec, state_spec],
        scratch_shapes=[pltpu.VMEM((stacked, first_rows), jnp.float32)],
        out_shape=[state_shape, state_shape, state_shape],
    )(queries, first_pos, first, first, extra, extra)
    return pl.pallas_call(
        functools.partial(second_kernel, per_device=per_device, stride=plane_rows[1]),
        grid=(head_count,),
        in_specs=[
            q_spec,
            pl.BlockSpec((1, second_rows), lambda h: (0, 0)),
            key_spec(second_rows),
            value_spec(second_rows),
            state_spec,
            state_spec,
            state_spec,
            pl.BlockSpec((rows, PICKS), lambda h: (0, 0)),
        ],
        out_specs=q_spec,
        scratch_shapes=[pltpu.VMEM((stacked, second_rows), jnp.float32)],
        out_shape=jax.ShapeDtypeStruct((rows, head_count * PICKS * HEAD_DIM), jnp.bfloat16),
    )(queries, second_pos, second, second, acc, top, total, gate_live)


def body(queries, suffix_kv, window_kv, sink_kv, lengths, group_ids, hidden_in, router, picks):
    row_count = queries.shape[0]
    head_count = suffix_kv.shape[2] // HEAD_DIM
    partial_value = jnp.dot(hidden_in, router, preferred_element_type=jnp.float32)
    logits = lax.psum(partial_value, "tp")
    experts = jnp.arange(logits.shape[1], dtype=jnp.int32)
    chosen = jnp.sum(
        jnp.where(picks[:, :, None] == experts[None, None, :], logits[:, None, :], 0.0), axis=2
    )
    gate_values = jax.nn.sigmoid(chosen - chosen[:, ::-1])
    z_count = lax.axis_size("z")
    plane_count = lax.axis_size("ylo") * lax.axis_size("x")
    z_me = lax.axis_index("z")
    plane_me = lax.axis_index("ylo") * lax.axis_size("x") + lax.axis_index("x")
    my_group = group_ids[z_me * plane_count + plane_me]
    length = lengths[0]
    is_live = jnp.arange(row_count, dtype=jnp.int32) < length
    gate_live = jnp.where(is_live[:, None], gate_values, 0.0)

    width = 2 * head_count * HEAD_DIM
    per_device = window_kv.shape[1]
    local = window_kv.reshape(window_kv.shape[0], per_device, width)
    def shifted(value, shift):
        pairs = [(j, (j + shift) % z_count) for j in range(z_count)]
        return lax.ppermute(value, "z", pairs)

    half = per_device // 2
    up = shifted(local, 1)
    down = shifted(local, z_count - 1)
    far_up = shifted(jnp.concatenate([down, local, up[:, :half]], axis=1), 3)
    far_down = shifted(jnp.concatenate([local, up, down[:, half:]], axis=1), z_count - 3)
    near_pieces = ((0, 0, per_device), (1, 0, per_device), (z_count - 1, 0, per_device))
    far_pieces = (
        (2, 0, per_device),
        (3, 0, per_device),
        (4, 0, half),
        (z_count - 3, 0, per_device),
        (z_count - 2, 0, per_device),
        (4, half, per_device - half),
    )
    part_pieces = (near_pieces, far_pieces)
    part_data = (jnp.concatenate([local, up, down], axis=1), jnp.concatenate([far_up, far_down], axis=1))
    peer_groups = lax.dynamic_slice_in_dim(group_ids, z_me * plane_count, plane_count)
    plane_ids = jnp.arange(plane_count, dtype=jnp.int32)
    parts = []
    positions = []
    for pieces, data in zip(part_pieces, part_data):
        outgoing = jnp.where((peer_groups == 0)[:, None, None], data[None, 0], data[None, 1])
        received = lax.all_to_all(
            outgoing, ("ylo", "x"), split_axis=0, concat_axis=0, tiled=True
        )
        parts.append(received.reshape(plane_count * data.shape[1], width))
        piece_pos = []
        for shift, first, count in pieces:
            z_of = (z_me - shift) % z_count
            rows_of = first + jnp.arange(count, dtype=jnp.int32)
            piece_pos.append(
                (z_of * plane_count + plane_ids[:, None]) * per_device + rows_of[None, :]
            )
        positions.append(jnp.concatenate(piece_pos, axis=1).reshape(-1))

    sink_rows = lax.dynamic_index_in_dim(sink_kv, my_group, 0, keepdims=False)
    sink_count = sink_rows.shape[0]
    extra_rows = 2 * row_count
    extra = jnp.concatenate(
        [
            suffix_kv.reshape(row_count, width),
            sink_rows.reshape(sink_count, width),
            jnp.zeros((extra_rows - row_count - sink_count, width), suffix_kv.dtype),
        ],
        axis=0,
    )
    key_pos = jnp.concatenate(positions).reshape(1, -1)
    plane_rows = tuple(data.shape[1] for data in part_data)
    return attend(
        queries, key_pos, parts, plane_rows, extra, gate_live, head_count, sink_count, per_device
    )


def solution(mesh):
    plane_ylo, plane_x = 2, 4
    z_count = mesh.shape["req"] // (plane_ylo * plane_x)
    devices = mesh.devices.reshape(z_count, plane_ylo, plane_x, mesh.shape["tp"])
    inner = jax.sharding.Mesh(devices, ("z", "ylo", "x", "tp"))
    req = ("z", "ylo", "x")
    return jax.shard_map(
        body,
        mesh=inner,
        in_specs=(
            P(req, "tp"),
            P(req, None, "tp"),
            P(None, req, None, "tp"),
            P(None, None, None, "tp"),
            P(req),
            P(),
            P(req, "tp"),
            P("tp", None),
            P(req, None),
        ),
        out_specs=P(req, "tp"),
        check_vma=False,
    )
```

```python
import functools
import math

import jax
import jax.numpy as jnp
from jax import lax
from jax.experimental import pallas as pl
from jax.experimental.pallas import tpu as pltpu
from jax.sharding import PartitionSpec as P

HEAD_DIM = 128
PICKS = 2
CHUNK = 512


def stacked_queries(q_ref):
    q = q_ref[...]
    return jnp.concatenate([q[:, :HEAD_DIM], q[:, HEAD_DIM:]], axis=0)


def window_scores(q_stack, pos_ref, wk_ref, score_ref, rows, per_device, stride, scale):
    stacked = q_stack.shape[0]
    query_pos = lax.broadcasted_iota(jnp.int32, (stacked, 1), 0) % rows
    nt = (((1,), (1,)), ((), ()))
    top = jnp.full((stacked, 1), -jnp.inf, jnp.float32)
    for c in range(wk_ref.shape[0] // CHUNK):
        keys = wk_ref[pl.ds(c * CHUNK, CHUNK), :]
        s = lax.dot_general(q_stack, keys, nt, preferred_element_type=jnp.float32) * scale
        if (c * CHUNK) // stride * per_device < rows:
            key_pos = pos_ref[:, pl.ds(c * CHUNK, CHUNK)]
            s = jnp.where(key_pos > query_pos, s, -jnp.inf)
        score_ref[:, pl.ds(c * CHUNK, CHUNK)] = s
        top = jnp.maximum(top, jnp.max(s, axis=1, keepdims=True))
    return top


def window_sums(wv_ref, score_ref, top, total, acc):
    for c in range(wv_ref.shape[0] // CHUNK):
        e = jnp.exp(score_ref[:, pl.ds(c * CHUNK, CHUNK)] - top)
        total = total + jnp.sum(e, axis=1, keepdims=True)
        acc = acc + jnp.dot(
            e.astype(jnp.bfloat16),
            wv_ref[pl.ds(c * CHUNK, CHUNK), :],
            preferred_element_type=jnp.float32,
        )
    return total, acc


def first_kernel(
    q_ref,
    pos_ref,
    wk_ref,
    wv_ref,
    xk_ref,
    xv_ref,
    acc_ref,
    top_ref,
    total_ref,
    score_ref,
    *,
    extra_sinks,
    per_device,
    stride,
):
    rows = q_ref.shape[0]
    scale = 1.0 / math.sqrt(HEAD_DIM)
    q_stack = stacked_queries(q_ref)
    stacked = q_stack.shape[0]
    nt = (((1,), (1,)), ((), ()))
    extra_rows = xk_ref.shape[0]
    extra = (
        lax.dot_general(q_stack, xk_ref[...], nt, preferred_element_type=jnp.float32) * scale
    )
    extra_pos = lax.broadcasted_iota(jnp.int32, (stacked, extra_rows), 0) % rows
    extra_key = lax.broadcasted_iota(jnp.int32, (stacked, extra_rows), 1)
    extra_visible = (extra_key <= extra_pos) | (
        (extra_key >= rows) & (extra_key < rows + extra_sinks)
    )
    extra = jnp.where(extra_visible, extra, -jnp.inf)
    top = jnp.maximum(
        jnp.max(extra, axis=1, keepdims=True),
        window_scores(q_stack, pos_ref, wk_ref, score_ref, rows, per_device, stride, scale),
    )
    e = jnp.exp(extra - top)
    total = jnp.sum(e, axis=1, keepdims=True)
    acc = jnp.dot(e.astype(jnp.bfloat16), xv_ref[...], preferred_element_type=jnp.float32)
    total, acc = window_sums(wv_ref, score_ref, top, total, acc)
    acc_ref[...] = acc
    top_ref[...] = jnp.broadcast_to(top, top_ref.shape)
    total_ref[...] = jnp.broadcast_to(total, total_ref.shape)


def second_kernel(
    q_ref,
    pos_ref,
    wk_ref,
    wv_ref,
    acc_ref,
    top_ref,
    total_ref,
    gate_ref,
    out_ref,
    score_ref,
    *,
    per_device,
    stride,
):
    rows = q_ref.shape[0]
    scale = 1.0 / math.sqrt(HEAD_DIM)
    q_stack = stacked_queries(q_ref)
    first_top = top_ref[:, 0:1]
    top = jnp.maximum(
        first_top,
        window_scores(q_stack, pos_ref, wk_ref, score_ref, rows, per_device, stride, scale),
    )
    factor = jnp.exp(first_top - top)
    total, acc = window_sums(
        wv_ref, score_ref, top, total_ref[:, 0:1] * factor, acc_ref[...] * factor
    )
    attended = acc / total
    gate = gate_ref[...]
    out_ref[:, :HEAD_DIM] = (attended[:rows] * gate[:, 0:1]).astype(out_ref.dtype)
    out_ref[:, HEAD_DIM:] = (attended[rows:] * gate[:, 1:2]).astype(out_ref.dtype)


def attend_first(queries, key_pos, parts, plane_rows, extra, head_count, extra_sinks, per_device):
    rows = queries.shape[0]
    stacked = PICKS * rows
    extra_rows = extra.shape[0]
    first, second = parts
    first_rows = first.shape[0]
    second_rows = second.shape[0]
    first_pos = key_pos[:, :first_rows]
    second_pos = key_pos[:, first_rows:]
    q_spec = pl.BlockSpec((rows, PICKS * HEAD_DIM), lambda h: (0, h))
    state_spec = pl.BlockSpec((None, stacked, HEAD_DIM), lambda h: (h, 0, 0))
    state_shape = jax.ShapeDtypeStruct((head_count, stacked, HEAD_DIM), jnp.float32)

    def key_spec(part_rows):
        return pl.BlockSpec((part_rows, HEAD_DIM), lambda h: (0, h))

    def value_spec(part_rows):
        return pl.BlockSpec((part_rows, HEAD_DIM), lambda h: (0, head_count + h))

    acc, top, total = pl.pallas_call(
        functools.partial(
            first_kernel, extra_sinks=extra_sinks, per_device=per_device, stride=plane_rows[0]
        ),
        grid=(head_count,),
        in_specs=[
            q_spec,
            pl.BlockSpec((1, first_rows), lambda h: (0, 0)),
            key_spec(first_rows),
            value_spec(first_rows),
            key_spec(extra_rows),
            value_spec(extra_rows),
        ],
        out_specs=[state_spec, state_spec, state_spec],
        scratch_shapes=[pltpu.VMEM((stacked, first_rows), jnp.float32)],
        out_shape=[state_shape, state_shape, state_shape],
    )(queries, first_pos, first, first, extra, extra)
    return acc, top, total


def attend_second(queries, key_pos, parts, plane_rows, state, gate_live, head_count, per_device):
    rows = queries.shape[0]
    stacked = PICKS * rows
    first, second = parts
    first_rows = first.shape[0]
    second_rows = second.shape[0]
    second_pos = key_pos[:, first_rows:]
    acc, top, total = state
    q_spec = pl.BlockSpec((rows, PICKS * HEAD_DIM), lambda h: (0, h))
    state_spec = pl.BlockSpec((None, stacked, HEAD_DIM), lambda h: (h, 0, 0))

    def key_spec(part_rows):
        return pl.BlockSpec((part_rows, HEAD_DIM), lambda h: (0, h))

    def value_spec(part_rows):
        return pl.BlockSpec((part_rows, HEAD_DIM), lambda h: (0, head_count + h))

    return pl.pallas_call(
        functools.partial(second_kernel, per_device=per_device, stride=plane_rows[1]),
        grid=(head_count,),
        in_specs=[
            q_spec,
            pl.BlockSpec((1, second_rows), lambda h: (0, 0)),
            key_spec(second_rows),
            value_spec(second_rows),
            state_spec,
            state_spec,
            state_spec,
            pl.BlockSpec((rows, PICKS), lambda h: (0, 0)),
        ],
        out_specs=q_spec,
        scratch_shapes=[pltpu.VMEM((stacked, second_rows), jnp.float32)],
        out_shape=jax.ShapeDtypeStruct((rows, head_count * PICKS * HEAD_DIM), jnp.bfloat16),
    )(queries, second_pos, second, second, acc, top, total, gate_live)


def body(queries, suffix_kv, window_kv, sink_kv, lengths, group_ids, hidden_in, router, picks):
    row_count = queries.shape[0]
    head_count = suffix_kv.shape[2] // HEAD_DIM
    partial_value = jnp.dot(hidden_in, router, preferred_element_type=jnp.float32)
    z_count = lax.axis_size("z")
    plane_count = lax.axis_size("ylo") * lax.axis_size("x")
    z_me = lax.axis_index("z")
    plane_me = lax.axis_index("ylo") * lax.axis_size("x") + lax.axis_index("x")
    my_group = group_ids[z_me * plane_count + plane_me]

    width = 2 * head_count * HEAD_DIM
    per_device = window_kv.shape[1]
    local = window_kv.reshape(window_kv.shape[0], per_device, width)
    def shifted(value, shift):
        pairs = [(j, (j + shift) % z_count) for j in range(z_count)]
        return lax.ppermute(value, "z", pairs)

    half = per_device // 2
    up = shifted(local, 1)
    down = shifted(local, z_count - 1)
    far_up = shifted(jnp.concatenate([down, local, up[:, :half]], axis=1), 3)
    far_down = shifted(jnp.concatenate([local, up, down[:, half:]], axis=1), z_count - 3)
    near_pieces = ((0, 0, per_device), (1, 0, per_device), (z_count - 1, 0, per_device))
    far_pieces = (
        (2, 0, per_device),
        (3, 0, per_device),
        (4, 0, half),
        (z_count - 3, 0, per_device),
        (z_count - 2, 0, per_device),
        (4, half, per_device - half),
    )
    part_pieces = (near_pieces, far_pieces)
    part_data = (jnp.concatenate([local, up, down], axis=1), jnp.concatenate([far_up, far_down], axis=1))
    peer_groups = lax.dynamic_slice_in_dim(group_ids, z_me * plane_count, plane_count)
    plane_ids = jnp.arange(plane_count, dtype=jnp.int32)
    parts = []
    positions = []
    for pieces, data in zip(part_pieces, part_data):
        outgoing = jnp.where((peer_groups == 0)[:, None, None], data[None, 0], data[None, 1])
        received = lax.all_to_all(
            outgoing, ("ylo", "x"), split_axis=0, concat_axis=0, tiled=True
        )
        parts.append(received.reshape(plane_count * data.shape[1], width))
        piece_pos = []
        for shift, first, count in pieces:
            z_of = (z_me - shift) % z_count
            rows_of = first + jnp.arange(count, dtype=jnp.int32)
            piece_pos.append(
                (z_of * plane_count + plane_ids[:, None]) * per_device + rows_of[None, :]
            )
        positions.append(jnp.concatenate(piece_pos, axis=1).reshape(-1))

    sink_rows = lax.dynamic_index_in_dim(sink_kv, my_group, 0, keepdims=False)
    sink_count = sink_rows.shape[0]
    extra_rows = 2 * row_count
    extra = jnp.concatenate(
        [
            suffix_kv.reshape(row_count, width),
            sink_rows.reshape(sink_count, width),
            jnp.zeros((extra_rows - row_count - sink_count, width), suffix_kv.dtype),
        ],
        axis=0,
    )
    key_pos = jnp.concatenate(positions).reshape(1, -1)
    plane_rows = tuple(data.shape[1] for data in part_data)
    state = attend_first(queries, key_pos, parts, plane_rows, extra, head_count, sink_count, per_device)
    state, partial_value = lax.optimization_barrier((state, partial_value))
    logits = lax.psum(partial_value, "tp")
    experts = jnp.arange(logits.shape[1], dtype=jnp.int32)
    chosen = jnp.sum(
        jnp.where(picks[:, :, None] == experts[None, None, :], logits[:, None, :], 0.0), axis=2
    )
    gate_values = jax.nn.sigmoid(chosen - chosen[:, ::-1])
    is_live = jnp.arange(row_count, dtype=jnp.int32) < lengths[0]
    gate_live = jnp.where(is_live[:, None], gate_values, 0.0)
    return attend_second(
        queries, key_pos, parts, plane_rows, state, gate_live, head_count, per_device
    )


def solution(mesh):
    plane_ylo, plane_x = 2, 4
    z_count = mesh.shape["req"] // (plane_ylo * plane_x)
    devices = mesh.devices.reshape(z_count, plane_ylo, plane_x, mesh.shape["tp"])
    inner = jax.sharding.Mesh(devices, ("z", "ylo", "x", "tp"))
    req = ("z", "ylo", "x")
    return jax.shard_map(
        body,
        mesh=inner,
        in_specs=(
            P(req, "tp"),
            P(req, None, "tp"),
            P(None, req, None, "tp"),
            P(None, None, None, "tp"),
            P(req),
            P(),
            P(req, "tp"),
            P("tp", None),
            P(req, None),
        ),
        out_specs=P(req, "tp"),
        check_vma=False,
    )
```

```python
import functools
import math

import jax
import jax.numpy as jnp
from jax import lax
from jax.experimental import pallas as pl
from jax.experimental.pallas import tpu as pltpu
from jax.sharding import PartitionSpec as P

HEAD_DIM = 128
PICKS = 2
CHUNK = 512


def stacked_queries(q_ref):
    q = q_ref[...]
    return jnp.concatenate([q[:, :HEAD_DIM], q[:, HEAD_DIM:]], axis=0)


def window_scores(q_stack, pos_ref, wk_ref, score_ref, rows, per_device, stride, scale):
    stacked = q_stack.shape[0]
    query_pos = lax.broadcasted_iota(jnp.int32, (stacked, 1), 0) % rows
    nt = (((1,), (1,)), ((), ()))
    top = jnp.full((stacked, 1), -jnp.inf, jnp.float32)
    for c in range(wk_ref.shape[0] // CHUNK):
        keys = wk_ref[pl.ds(c * CHUNK, CHUNK), :]
        s = lax.dot_general(q_stack, keys, nt, preferred_element_type=jnp.float32) * scale
        if (c * CHUNK) // stride * per_device < rows:
            key_pos = pos_ref[:, pl.ds(c * CHUNK, CHUNK)]
            s = jnp.where(key_pos > query_pos, s, -jnp.inf)
        score_ref[:, pl.ds(c * CHUNK, CHUNK)] = s
        top = jnp.maximum(top, jnp.max(s, axis=1, keepdims=True))
    return top


def window_sums(wv_ref, score_ref, top, total, acc):
    for c in range(wv_ref.shape[0] // CHUNK):
        e = jnp.exp(score_ref[:, pl.ds(c * CHUNK, CHUNK)] - top)
        total = total + jnp.sum(e, axis=1, keepdims=True)
        acc = acc + jnp.dot(
            e.astype(jnp.bfloat16),
            wv_ref[pl.ds(c * CHUNK, CHUNK), :],
            preferred_element_type=jnp.float32,
        )
    return total, acc


def first_kernel(
    q_ref,
    pos_ref,
    wk_ref,
    wv_ref,
    xk_ref,
    xv_ref,
    acc_ref,
    top_ref,
    total_ref,
    score_ref,
    *,
    extra_sinks,
    per_device,
    stride,
):
    rows = q_ref.shape[0]
    scale = 1.0 / math.sqrt(HEAD_DIM)
    q_stack = stacked_queries(q_ref)
    stacked = q_stack.shape[0]
    nt = (((1,), (1,)), ((), ()))
    extra_rows = xk_ref.shape[0]
    extra = (
        lax.dot_general(q_stack, xk_ref[...], nt, preferred_element_type=jnp.float32) * scale
    )
    extra_pos = lax.broadcasted_iota(jnp.int32, (stacked, extra_rows), 0) % rows
    extra_key = lax.broadcasted_iota(jnp.int32, (stacked, extra_rows), 1)
    extra_visible = (extra_key <= extra_pos) | (
        (extra_key >= rows) & (extra_key < rows + extra_sinks)
    )
    extra = jnp.where(extra_visible, extra, -jnp.inf)
    top = jnp.maximum(
        jnp.max(extra, axis=1, keepdims=True),
        window_scores(q_stack, pos_ref, wk_ref, score_ref, rows, per_device, stride, scale),
    )
    e = jnp.exp(extra - top)
    total = jnp.sum(e, axis=1, keepdims=True)
    acc = jnp.dot(e.astype(jnp.bfloat16), xv_ref[...], preferred_element_type=jnp.float32)
    total, acc = window_sums(wv_ref, score_ref, top, total, acc)
    acc_ref[...] = acc
    top_ref[...] = jnp.broadcast_to(top, top_ref.shape)
    total_ref[...] = jnp.broadcast_to(total, total_ref.shape)


def second_kernel(
    q_ref,
    pos_ref,
    wk_ref,
    wv_ref,
    acc_ref,
    top_ref,
    total_ref,
    logits_ref,
    pick0_ref,
    pick1_ref,
    live_ref,
    out_ref,
    score_ref,
    *,
    per_device,
    stride,
):
    rows = q_ref.shape[0]
    scale = 1.0 / math.sqrt(HEAD_DIM)
    q_stack = stacked_queries(q_ref)
    first_top = top_ref[:, 0:1]
    top = jnp.maximum(
        first_top,
        window_scores(q_stack, pos_ref, wk_ref, score_ref, rows, per_device, stride, scale),
    )
    factor = jnp.exp(first_top - top)
    total, acc = window_sums(
        wv_ref, score_ref, top, total_ref[:, 0:1] * factor, acc_ref[...] * factor
    )
    attended = acc / total
    logits = logits_ref[...]
    chosen0 = jnp.sum(jnp.where(pick0_ref[...] != 0, logits, 0.0), axis=1, keepdims=True)
    chosen1 = jnp.sum(jnp.where(pick1_ref[...] != 0, logits, 0.0), axis=1, keepdims=True)
    live = live_ref[...] != 0
    gate0 = jnp.where(live, jax.nn.sigmoid(chosen0 - chosen1), 0.0)
    gate1 = jnp.where(live, jax.nn.sigmoid(chosen1 - chosen0), 0.0)
    out_ref[:, :HEAD_DIM] = (attended[:rows] * gate0).astype(out_ref.dtype)
    out_ref[:, HEAD_DIM:] = (attended[rows:] * gate1).astype(out_ref.dtype)


def attend_first(queries, key_pos, parts, plane_rows, extra, head_count, extra_sinks, per_device):
    rows = queries.shape[0]
    stacked = PICKS * rows
    extra_rows = extra.shape[0]
    first, second = parts
    first_rows = first.shape[0]
    second_rows = second.shape[0]
    first_pos = key_pos[:, :first_rows]
    second_pos = key_pos[:, first_rows:]
    q_spec = pl.BlockSpec((rows, PICKS * HEAD_DIM), lambda h: (0, h))
    state_spec = pl.BlockSpec((None, stacked, HEAD_DIM), lambda h: (h, 0, 0))
    state_shape = jax.ShapeDtypeStruct((head_count, stacked, HEAD_DIM), jnp.float32)

    def key_spec(part_rows):
        return pl.BlockSpec((part_rows, HEAD_DIM), lambda h: (0, h))

    def value_spec(part_rows):
        return pl.BlockSpec((part_rows, HEAD_DIM), lambda h: (0, head_count + h))

    acc, top, total = pl.pallas_call(
        functools.partial(
            first_kernel, extra_sinks=extra_sinks, per_device=per_device, stride=plane_rows[0]
        ),
        grid=(head_count,),
        in_specs=[
            q_spec,
            pl.BlockSpec((1, first_rows), lambda h: (0, 0)),
            key_spec(first_rows),
            value_spec(first_rows),
            key_spec(extra_rows),
            value_spec(extra_rows),
        ],
        out_specs=[state_spec, state_spec, state_spec],
        scratch_shapes=[pltpu.VMEM((stacked, first_rows), jnp.float32)],
        out_shape=[state_shape, state_shape, state_shape],
    )(queries, first_pos, first, first, extra, extra)
    return acc, top, total


def attend_second(queries, key_pos, parts, plane_rows, state, gate_inputs, head_count, per_device):
    rows = queries.shape[0]
    stacked = PICKS * rows
    first, second = parts
    first_rows = first.shape[0]
    second_rows = second.shape[0]
    second_pos = key_pos[:, first_rows:]
    acc, top, total = state
    q_spec = pl.BlockSpec((rows, PICKS * HEAD_DIM), lambda h: (0, h))
    state_spec = pl.BlockSpec((None, stacked, HEAD_DIM), lambda h: (h, 0, 0))

    def key_spec(part_rows):
        return pl.BlockSpec((part_rows, HEAD_DIM), lambda h: (0, h))

    def value_spec(part_rows):
        return pl.BlockSpec((part_rows, HEAD_DIM), lambda h: (0, head_count + h))

    return pl.pallas_call(
        functools.partial(second_kernel, per_device=per_device, stride=plane_rows[1]),
        grid=(head_count,),
        in_specs=[
            q_spec,
            pl.BlockSpec((1, second_rows), lambda h: (0, 0)),
            key_spec(second_rows),
            value_spec(second_rows),
            state_spec,
            state_spec,
            state_spec,
        ]
        + [pl.BlockSpec(value.shape, lambda h: (0, 0)) for value in gate_inputs],
        out_specs=q_spec,
        scratch_shapes=[pltpu.VMEM((stacked, second_rows), jnp.float32)],
        out_shape=jax.ShapeDtypeStruct((rows, head_count * PICKS * HEAD_DIM), jnp.bfloat16),
    )(queries, second_pos, second, second, acc, top, total, *gate_inputs)


def body(queries, suffix_kv, window_kv, sink_kv, lengths, group_ids, hidden_in, router, picks):
    row_count = queries.shape[0]
    head_count = suffix_kv.shape[2] // HEAD_DIM
    partial_value = jnp.dot(hidden_in, router, preferred_element_type=jnp.float32)
    z_count = lax.axis_size("z")
    plane_count = lax.axis_size("ylo") * lax.axis_size("x")
    z_me = lax.axis_index("z")
    plane_me = lax.axis_index("ylo") * lax.axis_size("x") + lax.axis_index("x")
    my_group = group_ids[z_me * plane_count + plane_me]

    width = 2 * head_count * HEAD_DIM
    per_device = window_kv.shape[1]
    local = window_kv.reshape(window_kv.shape[0], per_device, width)
    def shifted(value, shift):
        pairs = [(j, (j + shift) % z_count) for j in range(z_count)]
        return lax.ppermute(value, "z", pairs)

    half = per_device // 2
    up = shifted(local, 1)
    down = shifted(local, z_count - 1)
    far_up = shifted(jnp.concatenate([down, local, up[:, :half]], axis=1), 3)
    far_down = shifted(jnp.concatenate([local, up, down[:, half:]], axis=1), z_count - 3)
    near_pieces = ((0, 0, per_device), (1, 0, per_device), (z_count - 1, 0, per_device))
    far_pieces = (
        (2, 0, per_device),
        (3, 0, per_device),
        (4, 0, half),
        (z_count - 3, 0, per_device),
        (z_count - 2, 0, per_device),
        (4, half, per_device - half),
    )
    part_pieces = (near_pieces, far_pieces)
    part_data = (jnp.concatenate([local, up, down], axis=1), jnp.concatenate([far_up, far_down], axis=1))
    peer_groups = lax.dynamic_slice_in_dim(group_ids, z_me * plane_count, plane_count)
    plane_ids = jnp.arange(plane_count, dtype=jnp.int32)
    parts = []
    positions = []
    for pieces, data in zip(part_pieces, part_data):
        outgoing = jnp.where((peer_groups == 0)[:, None, None], data[None, 0], data[None, 1])
        received = lax.all_to_all(
            outgoing, ("ylo", "x"), split_axis=0, concat_axis=0, tiled=True
        )
        parts.append(received.reshape(plane_count * data.shape[1], width))
        piece_pos = []
        for shift, first, count in pieces:
            z_of = (z_me - shift) % z_count
            rows_of = first + jnp.arange(count, dtype=jnp.int32)
            piece_pos.append(
                (z_of * plane_count + plane_ids[:, None]) * per_device + rows_of[None, :]
            )
        positions.append(jnp.concatenate(piece_pos, axis=1).reshape(-1))

    sink_rows = lax.dynamic_index_in_dim(sink_kv, my_group, 0, keepdims=False)
    sink_count = sink_rows.shape[0]
    extra_rows = 2 * row_count
    extra = jnp.concatenate(
        [
            suffix_kv.reshape(row_count, width),
            sink_rows.reshape(sink_count, width),
            jnp.zeros((extra_rows - row_count - sink_count, width), suffix_kv.dtype),
        ],
        axis=0,
    )
    key_pos = jnp.concatenate(positions).reshape(1, -1)
    plane_rows = tuple(data.shape[1] for data in part_data)
    state = attend_first(queries, key_pos, parts, plane_rows, extra, head_count, sink_count, per_device)
    state, partial_value = lax.optimization_barrier((state, partial_value))
    logits = lax.psum(partial_value, "tp")
    experts = jnp.arange(logits.shape[1], dtype=jnp.int32)
    pick0 = (picks[:, 0:1] == experts[None, :]).astype(jnp.int32)
    pick1 = (picks[:, 1:2] == experts[None, :]).astype(jnp.int32)
    is_live = (jnp.arange(row_count, dtype=jnp.int32) < lengths[0]).astype(jnp.int32)
    gate_inputs = (logits, pick0, pick1, is_live[:, None])
    return attend_second(
        queries, key_pos, parts, plane_rows, state, gate_inputs, head_count, per_device
    )


def solution(mesh):
    plane_ylo, plane_x = 2, 4
    z_count = mesh.shape["req"] // (plane_ylo * plane_x)
    devices = mesh.devices.reshape(z_count, plane_ylo, plane_x, mesh.shape["tp"])
    inner = jax.sharding.Mesh(devices, ("z", "ylo", "x", "tp"))
    req = ("z", "ylo", "x")
    return jax.shard_map(
        body,
        mesh=inner,
        in_specs=(
            P(req, "tp"),
            P(req, None, "tp"),
            P(None, req, None, "tp"),
            P(None, None, None, "tp"),
            P(req),
            P(),
            P(req, "tp"),
            P("tp", None),
            P(req, None),
        ),
        out_specs=P(req, "tp"),
        check_vma=False,
    )
```

```python
import functools
import math

import jax
import jax.numpy as jnp
from jax import lax
from jax.experimental import pallas as pl
from jax.experimental.pallas import tpu as pltpu
from jax.sharding import PartitionSpec as P

HEAD_DIM = 128
PICKS = 2
CHUNK = 512


def stacked_queries(q_ref):
    q = q_ref[...]
    return jnp.concatenate([q[:, :HEAD_DIM], q[:, HEAD_DIM:]], axis=0)


def window_scores(q_stack, pos_ref, wk_ref, score_ref, rows, per_device, stride, scale):
    stacked = q_stack.shape[0]
    query_pos = lax.broadcasted_iota(jnp.int32, (stacked, 1), 0) % rows
    nt = (((1,), (1,)), ((), ()))
    top = jnp.full((stacked, 1), -jnp.inf, jnp.float32)
    for c in range(wk_ref.shape[0] // CHUNK):
        keys = wk_ref[pl.ds(c * CHUNK, CHUNK), :]
        s = lax.dot_general(q_stack, keys, nt, preferred_element_type=jnp.float32) * scale
        if (c * CHUNK) // stride * per_device < rows:
            key_pos = pos_ref[:, pl.ds(c * CHUNK, CHUNK)]
            s = jnp.where(key_pos > query_pos, s, -jnp.inf)
        score_ref[:, pl.ds(c * CHUNK, CHUNK)] = s
        top = jnp.maximum(top, jnp.max(s, axis=1, keepdims=True))
    return top


def window_sums(wv_ref, score_ref, top, total, acc):
    for c in range(wv_ref.shape[0] // CHUNK):
        e = jnp.exp(score_ref[:, pl.ds(c * CHUNK, CHUNK)] - top)
        total = total + jnp.sum(e, axis=1, keepdims=True)
        acc = acc + jnp.dot(
            e.astype(jnp.bfloat16),
            wv_ref[pl.ds(c * CHUNK, CHUNK), :],
            preferred_element_type=jnp.float32,
        )
    return total, acc


def first_kernel(
    q_ref,
    pos_ref,
    wk_ref,
    wv_ref,
    xk_ref,
    xv_ref,
    acc_ref,
    top_ref,
    total_ref,
    score_ref,
    *,
    extra_sinks,
    per_device,
    stride,
):
    rows = q_ref.shape[0]
    scale = 1.0 / math.sqrt(HEAD_DIM)
    q_stack = stacked_queries(q_ref)
    stacked = q_stack.shape[0]
    nt = (((1,), (1,)), ((), ()))
    extra_rows = xk_ref.shape[0]
    extra = (
        lax.dot_general(q_stack, xk_ref[...], nt, preferred_element_type=jnp.float32) * scale
    )
    extra_pos = lax.broadcasted_iota(jnp.int32, (stacked, extra_rows), 0) % rows
    extra_key = lax.broadcasted_iota(jnp.int32, (stacked, extra_rows), 1)
    extra_visible = (extra_key <= extra_pos) | (
        (extra_key >= rows) & (extra_key < rows + extra_sinks)
    )
    extra = jnp.where(extra_visible, extra, -jnp.inf)
    top = jnp.maximum(
        jnp.max(extra, axis=1, keepdims=True),
        window_scores(q_stack, pos_ref, wk_ref, score_ref, rows, per_device, stride, scale),
    )
    e = jnp.exp(extra - top)
    total = jnp.sum(e, axis=1, keepdims=True)
    acc = jnp.dot(e.astype(jnp.bfloat16), xv_ref[...], preferred_element_type=jnp.float32)
    total, acc = window_sums(wv_ref, score_ref, top, total, acc)
    acc_ref[...] = acc
    top_ref[...] = jnp.broadcast_to(top, top_ref.shape)
    total_ref[...] = jnp.broadcast_to(total, total_ref.shape)


def second_kernel(
    q_ref,
    pos_ref,
    wk_ref,
    wv_ref,
    acc_ref,
    top_ref,
    total_ref,
    logits_ref,
    pick0_ref,
    pick1_ref,
    live_ref,
    out_ref,
    score_ref,
    *,
    per_device,
    stride,
):
    rows = q_ref.shape[0]
    scale = 1.0 / math.sqrt(HEAD_DIM)
    q_stack = stacked_queries(q_ref)
    first_top = top_ref[:, 0:1]
    top = jnp.maximum(
        first_top,
        window_scores(q_stack, pos_ref, wk_ref, score_ref, rows, per_device, stride, scale),
    )
    factor = jnp.exp(first_top - top)
    total, acc = window_sums(
        wv_ref, score_ref, top, total_ref[:, 0:1] * factor, acc_ref[...] * factor
    )
    attended = acc / total
    logits = logits_ref[...]
    chosen0 = jnp.sum(jnp.where(pick0_ref[...] != 0, logits, 0.0), axis=0, keepdims=True)
    chosen1 = jnp.sum(jnp.where(pick1_ref[...] != 0, logits, 0.0), axis=0, keepdims=True)
    live = live_ref[...] != 0
    gate_rows = jnp.concatenate(
        [
            jnp.where(live, jax.nn.sigmoid(chosen0 - chosen1), 0.0),
            jnp.where(live, jax.nn.sigmoid(chosen1 - chosen0), 0.0),
            jnp.zeros((logits.shape[0] - PICKS, logits.shape[1]), jnp.float32),
        ],
        axis=0,
    )
    gate_cols = jnp.transpose(gate_rows)
    gate0 = gate_cols[:, 0:1]
    gate1 = gate_cols[:, 1:2]
    out_ref[:, :HEAD_DIM] = (attended[:rows] * gate0).astype(out_ref.dtype)
    out_ref[:, HEAD_DIM:] = (attended[rows:] * gate1).astype(out_ref.dtype)


def attend_first(queries, key_pos, parts, plane_rows, extra, head_count, extra_sinks, per_device):
    rows = queries.shape[0]
    stacked = PICKS * rows
    extra_rows = extra.shape[0]
    first, second = parts
    first_rows = first.shape[0]
    second_rows = second.shape[0]
    first_pos = key_pos[:, :first_rows]
    second_pos = key_pos[:, first_rows:]
    q_spec = pl.BlockSpec((rows, PICKS * HEAD_DIM), lambda h: (0, h))
    state_spec = pl.BlockSpec((None, stacked, HEAD_DIM), lambda h: (h, 0, 0))
    state_shape = jax.ShapeDtypeStruct((head_count, stacked, HEAD_DIM), jnp.float32)

    def key_spec(part_rows):
        return pl.BlockSpec((part_rows, HEAD_DIM), lambda h: (0, h))

    def value_spec(part_rows):
        return pl.BlockSpec((part_rows, HEAD_DIM), lambda h: (0, head_count + h))

    acc, top, total = pl.pallas_call(
        functools.partial(
            first_kernel, extra_sinks=extra_sinks, per_device=per_device, stride=plane_rows[0]
        ),
        grid=(head_count,),
        in_specs=[
            q_spec,
            pl.BlockSpec((1, first_rows), lambda h: (0, 0)),
            key_spec(first_rows),
            value_spec(first_rows),
            key_spec(extra_rows),
            value_spec(extra_rows),
        ],
        out_specs=[state_spec, state_spec, state_spec],
        scratch_shapes=[pltpu.VMEM((stacked, first_rows), jnp.float32)],
        out_shape=[state_shape, state_shape, state_shape],
    )(queries, first_pos, first, first, extra, extra)
    return acc, top, total


def attend_second(queries, key_pos, parts, plane_rows, state, gate_inputs, head_count, per_device):
    rows = queries.shape[0]
    stacked = PICKS * rows
    first, second = parts
    first_rows = first.shape[0]
    second_rows = second.shape[0]
    second_pos = key_pos[:, first_rows:]
    acc, top, total = state
    q_spec = pl.BlockSpec((rows, PICKS * HEAD_DIM), lambda h: (0, h))
    state_spec = pl.BlockSpec((None, stacked, HEAD_DIM), lambda h: (h, 0, 0))

    def key_spec(part_rows):
        return pl.BlockSpec((part_rows, HEAD_DIM), lambda h: (0, h))

    def value_spec(part_rows):
        return pl.BlockSpec((part_rows, HEAD_DIM), lambda h: (0, head_count + h))

    return pl.pallas_call(
        functools.partial(second_kernel, per_device=per_device, stride=plane_rows[1]),
        grid=(head_count,),
        in_specs=[
            q_spec,
            pl.BlockSpec((1, second_rows), lambda h: (0, 0)),
            key_spec(second_rows),
            value_spec(second_rows),
            state_spec,
            state_spec,
            state_spec,
        ]
        + [pl.BlockSpec(value.shape, lambda h: (0, 0)) for value in gate_inputs],
        out_specs=q_spec,
        scratch_shapes=[pltpu.VMEM((stacked, second_rows), jnp.float32)],
        out_shape=jax.ShapeDtypeStruct((rows, head_count * PICKS * HEAD_DIM), jnp.bfloat16),
    )(queries, second_pos, second, second, acc, top, total, *gate_inputs)


def body(queries, suffix_kv, window_kv, sink_kv, lengths, group_ids, hidden_in, router, picks):
    row_count = queries.shape[0]
    head_count = suffix_kv.shape[2] // HEAD_DIM
    partial_value = jnp.dot(hidden_in, router, preferred_element_type=jnp.float32)
    z_count = lax.axis_size("z")
    plane_count = lax.axis_size("ylo") * lax.axis_size("x")
    z_me = lax.axis_index("z")
    plane_me = lax.axis_index("ylo") * lax.axis_size("x") + lax.axis_index("x")
    my_group = group_ids[z_me * plane_count + plane_me]

    width = 2 * head_count * HEAD_DIM
    per_device = window_kv.shape[1]
    local = window_kv.reshape(window_kv.shape[0], per_device, width)
    def shifted(value, shift):
        pairs = [(j, (j + shift) % z_count) for j in range(z_count)]
        return lax.ppermute(value, "z", pairs)

    half = per_device // 2
    up = shifted(local, 1)
    down = shifted(local, z_count - 1)
    far_up = shifted(jnp.concatenate([down, local, up[:, :half]], axis=1), 3)
    far_down = shifted(jnp.concatenate([local, up, down[:, half:]], axis=1), z_count - 3)
    near_pieces = ((0, 0, per_device), (1, 0, per_device), (z_count - 1, 0, per_device))
    far_pieces = (
        (2, 0, per_device),
        (3, 0, per_device),
        (4, 0, half),
        (z_count - 3, 0, per_device),
        (z_count - 2, 0, per_device),
        (4, half, per_device - half),
    )
    part_pieces = (near_pieces, far_pieces)
    part_data = (jnp.concatenate([local, up, down], axis=1), jnp.concatenate([far_up, far_down], axis=1))
    peer_groups = lax.dynamic_slice_in_dim(group_ids, z_me * plane_count, plane_count)
    plane_ids = jnp.arange(plane_count, dtype=jnp.int32)
    parts = []
    positions = []
    for pieces, data in zip(part_pieces, part_data):
        outgoing = jnp.where((peer_groups == 0)[:, None, None], data[None, 0], data[None, 1])
        received = lax.all_to_all(
            outgoing, ("ylo", "x"), split_axis=0, concat_axis=0, tiled=True
        )
        parts.append(received.reshape(plane_count * data.shape[1], width))
        piece_pos = []
        for shift, first, count in pieces:
            z_of = (z_me - shift) % z_count
            rows_of = first + jnp.arange(count, dtype=jnp.int32)
            piece_pos.append(
                (z_of * plane_count + plane_ids[:, None]) * per_device + rows_of[None, :]
            )
        positions.append(jnp.concatenate(piece_pos, axis=1).reshape(-1))

    sink_rows = lax.dynamic_index_in_dim(sink_kv, my_group, 0, keepdims=False)
    sink_count = sink_rows.shape[0]
    extra_rows = 2 * row_count
    extra = jnp.concatenate(
        [
            suffix_kv.reshape(row_count, width),
            sink_rows.reshape(sink_count, width),
            jnp.zeros((extra_rows - row_count - sink_count, width), suffix_kv.dtype),
        ],
        axis=0,
    )
    key_pos = jnp.concatenate(positions).reshape(1, -1)
    plane_rows = tuple(data.shape[1] for data in part_data)
    state = attend_first(queries, key_pos, parts, plane_rows, extra, head_count, sink_count, per_device)
    state, partial_value = lax.optimization_barrier((state, partial_value))
    logits = lax.psum(partial_value, "tp")
    experts = jnp.arange(logits.shape[1], dtype=jnp.int32)
    pick0 = (picks[:, 0][None, :] == experts[:, None]).astype(jnp.int32)
    pick1 = (picks[:, 1][None, :] == experts[:, None]).astype(jnp.int32)
    is_live = (jnp.arange(row_count, dtype=jnp.int32) < lengths[0]).astype(jnp.int32)
    gate_inputs = (jnp.transpose(logits), pick0, pick1, is_live[None, :])
    return attend_second(
        queries, key_pos, parts, plane_rows, state, gate_inputs, head_count, per_device
    )


def solution(mesh):
    plane_ylo, plane_x = 2, 4
    z_count = mesh.shape["req"] // (plane_ylo * plane_x)
    devices = mesh.devices.reshape(z_count, plane_ylo, plane_x, mesh.shape["tp"])
    inner = jax.sharding.Mesh(devices, ("z", "ylo", "x", "tp"))
    req = ("z", "ylo", "x")
    return jax.shard_map(
        body,
        mesh=inner,
        in_specs=(
            P(req, "tp"),
            P(req, None, "tp"),
            P(None, req, None, "tp"),
            P(None, None, None, "tp"),
            P(req),
            P(),
            P(req, "tp"),
            P("tp", None),
            P(req, None),
        ),
        out_specs=P(req, "tp"),
        check_vma=False,
    )
```

```python
import functools
import math

import jax
import jax.numpy as jnp
from jax import lax
from jax.experimental import pallas as pl
from jax.experimental.pallas import tpu as pltpu
from jax.sharding import PartitionSpec as P

HEAD_DIM = 128
PICKS = 2
CHUNK = 512


def stacked_queries(q_ref):
    q = q_ref[...]
    return jnp.concatenate([q[:, :HEAD_DIM], q[:, HEAD_DIM:]], axis=0)


def window_scores(q_stack, pos_ref, wk_ref, score_ref, rows, per_device, stride, scale):
    stacked = q_stack.shape[0]
    query_pos = lax.broadcasted_iota(jnp.int32, (stacked, 1), 0) % rows
    nt = (((1,), (1,)), ((), ()))
    top = jnp.full((stacked, 1), -jnp.inf, jnp.float32)
    for c in range(wk_ref.shape[0] // CHUNK):
        keys = wk_ref[pl.ds(c * CHUNK, CHUNK), :]
        s = lax.dot_general(q_stack, keys, nt, preferred_element_type=jnp.float32) * scale
        if stride is None or (c * CHUNK) // stride * per_device < rows:
            key_pos = pos_ref[:, pl.ds(c * CHUNK, CHUNK)]
            s = jnp.where(key_pos > query_pos, s, -jnp.inf)
        score_ref[:, pl.ds(c * CHUNK, CHUNK)] = s
        top = jnp.maximum(top, jnp.max(s, axis=1, keepdims=True))
    return top


def window_sums(wv_ref, score_ref, top, total, acc):
    for c in range(wv_ref.shape[0] // CHUNK):
        e = jnp.exp(score_ref[:, pl.ds(c * CHUNK, CHUNK)] - top)
        total = total + jnp.sum(e, axis=1, keepdims=True)
        acc = acc + jnp.dot(
            e.astype(jnp.bfloat16),
            wv_ref[pl.ds(c * CHUNK, CHUNK), :],
            preferred_element_type=jnp.float32,
        )
    return total, acc


def first_kernel(
    q_ref,
    pos_ref,
    wk_ref,
    wv_ref,
    xk_ref,
    xv_ref,
    acc_ref,
    top_ref,
    total_ref,
    score_ref,
    *,
    extra_sinks,
    per_device,
    stride,
):
    rows = q_ref.shape[0]
    scale = 1.0 / math.sqrt(HEAD_DIM)
    q_stack = stacked_queries(q_ref)
    stacked = q_stack.shape[0]
    nt = (((1,), (1,)), ((), ()))
    extra_rows = xk_ref.shape[0]
    extra = (
        lax.dot_general(q_stack, xk_ref[...], nt, preferred_element_type=jnp.float32) * scale
    )
    extra_pos = lax.broadcasted_iota(jnp.int32, (stacked, extra_rows), 0) % rows
    extra_key = lax.broadcasted_iota(jnp.int32, (stacked, extra_rows), 1)
    extra_visible = (extra_key <= extra_pos) | (
        (extra_key >= rows) & (extra_key < rows + extra_sinks)
    )
    extra = jnp.where(extra_visible, extra, -jnp.inf)
    top = jnp.maximum(
        jnp.max(extra, axis=1, keepdims=True),
        window_scores(q_stack, pos_ref, wk_ref, score_ref, rows, per_device, stride, scale),
    )
    e = jnp.exp(extra - top)
    total = jnp.sum(e, axis=1, keepdims=True)
    acc = jnp.dot(e.astype(jnp.bfloat16), xv_ref[...], preferred_element_type=jnp.float32)
    total, acc = window_sums(wv_ref, score_ref, top, total, acc)
    acc_ref[...] = acc
    top_ref[...] = jnp.broadcast_to(top, top_ref.shape)
    total_ref[...] = jnp.broadcast_to(total, total_ref.shape)


def second_kernel(
    q_ref,
    pos_ref,
    wk_ref,
    wv_ref,
    acc_ref,
    top_ref,
    total_ref,
    logits_ref,
    pick0_ref,
    pick1_ref,
    live_ref,
    out_ref,
    score_ref,
    *,
    per_device,
    stride,
):
    rows = q_ref.shape[0]
    scale = 1.0 / math.sqrt(HEAD_DIM)
    q_stack = stacked_queries(q_ref)
    first_top = top_ref[:, 0:1]
    top = jnp.maximum(
        first_top,
        window_scores(q_stack, pos_ref, wk_ref, score_ref, rows, per_device, stride, scale),
    )
    factor = jnp.exp(first_top - top)
    total, acc = window_sums(
        wv_ref, score_ref, top, total_ref[:, 0:1] * factor, acc_ref[...] * factor
    )
    attended = acc / total
    logits = logits_ref[...]
    chosen0 = jnp.sum(jnp.where(pick0_ref[...] != 0, logits, 0.0), axis=0, keepdims=True)
    chosen1 = jnp.sum(jnp.where(pick1_ref[...] != 0, logits, 0.0), axis=0, keepdims=True)
    live = live_ref[...] != 0
    gate_rows = jnp.concatenate(
        [
            jnp.where(live, jax.nn.sigmoid(chosen0 - chosen1), 0.0),
            jnp.where(live, jax.nn.sigmoid(chosen1 - chosen0), 0.0),
            jnp.zeros((logits.shape[0] - PICKS, logits.shape[1]), jnp.float32),
        ],
        axis=0,
    )
    gate_cols = jnp.transpose(gate_rows)
    gate0 = gate_cols[:, 0:1]
    gate1 = gate_cols[:, 1:2]
    out_ref[:, :HEAD_DIM] = (attended[:rows] * gate0).astype(out_ref.dtype)
    out_ref[:, HEAD_DIM:] = (attended[rows:] * gate1).astype(out_ref.dtype)


def attend_first(queries, key_pos, parts, plane_rows, extra, head_count, extra_sinks, per_device):
    rows = queries.shape[0]
    stacked = PICKS * rows
    extra_rows = extra.shape[0]
    first, second = parts
    first_rows = first.shape[0]
    second_rows = second.shape[0]
    first_pos = key_pos[:, :first_rows]
    second_pos = key_pos[:, first_rows:]
    q_spec = pl.BlockSpec((rows, PICKS * HEAD_DIM), lambda h: (0, h))
    state_spec = pl.BlockSpec((None, stacked, HEAD_DIM), lambda h: (h, 0, 0))
    state_shape = jax.ShapeDtypeStruct((head_count, stacked, HEAD_DIM), jnp.float32)

    def key_spec(part_rows):
        return pl.BlockSpec((part_rows, HEAD_DIM), lambda h: (0, h))

    def value_spec(part_rows):
        return pl.BlockSpec((part_rows, HEAD_DIM), lambda h: (0, head_count + h))

    acc, top, total = pl.pallas_call(
        functools.partial(
            first_kernel, extra_sinks=extra_sinks, per_device=per_device, stride=None
        ),
        grid=(head_count,),
        in_specs=[
            q_spec,
            pl.BlockSpec((1, first_rows), lambda h: (0, 0)),
            key_spec(first_rows),
            value_spec(first_rows),
            key_spec(extra_rows),
            value_spec(extra_rows),
        ],
        out_specs=[state_spec, state_spec, state_spec],
        scratch_shapes=[pltpu.VMEM((stacked, first_rows), jnp.float32)],
        out_shape=[state_shape, state_shape, state_shape],
    )(queries, first_pos, first, first, extra, extra)
    return acc, top, total


def attend_second(queries, key_pos, parts, plane_rows, state, gate_inputs, head_count, per_device):
    rows = queries.shape[0]
    stacked = PICKS * rows
    first, second = parts
    first_rows = first.shape[0]
    second_rows = second.shape[0]
    second_pos = key_pos[:, first_rows:]
    acc, top, total = state
    q_spec = pl.BlockSpec((rows, PICKS * HEAD_DIM), lambda h: (0, h))
    state_spec = pl.BlockSpec((None, stacked, HEAD_DIM), lambda h: (h, 0, 0))

    def key_spec(part_rows):
        return pl.BlockSpec((part_rows, HEAD_DIM), lambda h: (0, h))

    def value_spec(part_rows):
        return pl.BlockSpec((part_rows, HEAD_DIM), lambda h: (0, head_count + h))

    return pl.pallas_call(
        functools.partial(second_kernel, per_device=per_device, stride=plane_rows[1]),
        grid=(head_count,),
        in_specs=[
            q_spec,
            pl.BlockSpec((1, second_rows), lambda h: (0, 0)),
            key_spec(second_rows),
            value_spec(second_rows),
            state_spec,
            state_spec,
            state_spec,
        ]
        + [pl.BlockSpec(value.shape, lambda h: (0, 0)) for value in gate_inputs],
        out_specs=q_spec,
        scratch_shapes=[pltpu.VMEM((stacked, second_rows), jnp.float32)],
        out_shape=jax.ShapeDtypeStruct((rows, head_count * PICKS * HEAD_DIM), jnp.bfloat16),
    )(queries, second_pos, second, second, acc, top, total, *gate_inputs)


def body(queries, suffix_kv, window_kv, sink_kv, lengths, group_ids, hidden_in, router, picks):
    row_count = queries.shape[0]
    head_count = suffix_kv.shape[2] // HEAD_DIM
    partial_value = jnp.dot(hidden_in, router, preferred_element_type=jnp.float32)
    z_count = lax.axis_size("z")
    plane_count = lax.axis_size("ylo") * lax.axis_size("x")
    z_me = lax.axis_index("z")
    plane_me = lax.axis_index("ylo") * lax.axis_size("x") + lax.axis_index("x")
    my_group = group_ids[z_me * plane_count + plane_me]

    width = 2 * head_count * HEAD_DIM
    per_device = window_kv.shape[1]
    local = window_kv.reshape(window_kv.shape[0], per_device, width)
    def shifted(value, shift):
        pairs = [(j, (j + shift) % z_count) for j in range(z_count)]
        return lax.ppermute(value, "z", pairs)

    half = per_device // 2
    up = shifted(local, 1)
    down = shifted(local, z_count - 1)
    far_up = shifted(jnp.concatenate([down, local, up[:, :half]], axis=1), 3)
    far_down = shifted(jnp.concatenate([local, up, down[:, half:]], axis=1), z_count - 3)
    own_pieces = ((0, 0, per_device),)
    near_pieces = ((1, 0, per_device), (z_count - 1, 0, per_device))
    far_pieces = (
        (2, 0, per_device),
        (3, 0, per_device),
        (4, 0, half),
        (z_count - 3, 0, per_device),
        (z_count - 2, 0, per_device),
        (4, half, per_device - half),
    )
    part_pieces = (own_pieces, near_pieces, far_pieces)
    part_data = (
        local,
        jnp.concatenate([up, down], axis=1),
        jnp.concatenate([far_up, far_down], axis=1),
    )
    peer_groups = lax.dynamic_slice_in_dim(group_ids, z_me * plane_count, plane_count)
    plane_ids = jnp.arange(plane_count, dtype=jnp.int32)
    parts = []
    positions = []
    for pieces, data in zip(part_pieces, part_data):
        outgoing = jnp.where((peer_groups == 0)[:, None, None], data[None, 0], data[None, 1])
        received = lax.all_to_all(
            outgoing, ("ylo", "x"), split_axis=0, concat_axis=0, tiled=True
        )
        parts.append(received.reshape(plane_count * data.shape[1], width))
        piece_pos = []
        for shift, first, count in pieces:
            z_of = (z_me - shift) % z_count
            rows_of = first + jnp.arange(count, dtype=jnp.int32)
            piece_pos.append(
                (z_of * plane_count + plane_ids[:, None]) * per_device + rows_of[None, :]
            )
        positions.append(jnp.concatenate(piece_pos, axis=1).reshape(-1))

    sink_rows = lax.dynamic_index_in_dim(sink_kv, my_group, 0, keepdims=False)
    sink_count = sink_rows.shape[0]
    extra_rows = 2 * row_count
    extra = jnp.concatenate(
        [
            suffix_kv.reshape(row_count, width),
            sink_rows.reshape(sink_count, width),
            jnp.zeros((extra_rows - row_count - sink_count, width), suffix_kv.dtype),
        ],
        axis=0,
    )
    key_pos = jnp.concatenate(positions).reshape(1, -1)
    parts = [jnp.concatenate(parts[:2], axis=0), parts[2]]
    plane_rows = (None, part_data[2].shape[1])
    state = attend_first(queries, key_pos, parts, plane_rows, extra, head_count, sink_count, per_device)
    state, partial_value = lax.optimization_barrier((state, partial_value))
    logits = lax.psum(partial_value, "tp")
    experts = jnp.arange(logits.shape[1], dtype=jnp.int32)
    pick0 = (picks[:, 0][None, :] == experts[:, None]).astype(jnp.int32)
    pick1 = (picks[:, 1][None, :] == experts[:, None]).astype(jnp.int32)
    is_live = (jnp.arange(row_count, dtype=jnp.int32) < lengths[0]).astype(jnp.int32)
    gate_inputs = (jnp.transpose(logits), pick0, pick1, is_live[None, :])
    return attend_second(
        queries, key_pos, parts, plane_rows, state, gate_inputs, head_count, per_device
    )


def solution(mesh):
    plane_ylo, plane_x = 2, 4
    z_count = mesh.shape["req"] // (plane_ylo * plane_x)
    devices = mesh.devices.reshape(z_count, plane_ylo, plane_x, mesh.shape["tp"])
    inner = jax.sharding.Mesh(devices, ("z", "ylo", "x", "tp"))
    req = ("z", "ylo", "x")
    return jax.shard_map(
        body,
        mesh=inner,
        in_specs=(
            P(req, "tp"),
            P(req, None, "tp"),
            P(None, req, None, "tp"),
            P(None, None, None, "tp"),
            P(req),
            P(),
            P(req, "tp"),
            P("tp", None),
            P(req, None),
        ),
        out_specs=P(req, "tp"),
        check_vma=False,
    )
```

```python
import functools
import math

import jax
import jax.numpy as jnp
from jax import lax
from jax.experimental import pallas as pl
from jax.experimental.pallas import tpu as pltpu
from jax.sharding import PartitionSpec as P

HEAD_DIM = 128
PICKS = 2
CHUNK = 512


def stacked_queries(q_ref):
    q = q_ref[...]
    return jnp.concatenate([q[:, :HEAD_DIM], q[:, HEAD_DIM:]], axis=0)


def window_scores(q_stack, pos_ref, wk_ref, score_ref, rows, per_device, stride, scale):
    stacked = q_stack.shape[0]
    query_pos = lax.broadcasted_iota(jnp.int32, (stacked, 1), 0) % rows
    nt = (((1,), (1,)), ((), ()))
    lane_top = jnp.full((stacked, HEAD_DIM), -jnp.inf, jnp.float32)
    for c in range(wk_ref.shape[0] // CHUNK):
        keys = wk_ref[pl.ds(c * CHUNK, CHUNK), :]
        s = lax.dot_general(q_stack, keys, nt, preferred_element_type=jnp.float32) * scale
        if (c * CHUNK) // stride * per_device < rows:
            key_pos = pos_ref[:, pl.ds(c * CHUNK, CHUNK)]
            s = jnp.where(key_pos > query_pos, s, -jnp.inf)
        score_ref[:, pl.ds(c * CHUNK, CHUNK)] = s
        for j in range(CHUNK // HEAD_DIM):
            lane_top = jnp.maximum(lane_top, s[:, j * HEAD_DIM : (j + 1) * HEAD_DIM])
    return jnp.max(lane_top, axis=1, keepdims=True)


def window_sums(wv_ref, score_ref, top, total, acc):
    lane_total = jnp.zeros((top.shape[0], HEAD_DIM), jnp.float32)
    for c in range(wv_ref.shape[0] // CHUNK):
        e = jnp.exp(score_ref[:, pl.ds(c * CHUNK, CHUNK)] - top)
        for j in range(CHUNK // HEAD_DIM):
            lane_total = lane_total + e[:, j * HEAD_DIM : (j + 1) * HEAD_DIM]
        acc = acc + jnp.dot(
            e.astype(jnp.bfloat16),
            wv_ref[pl.ds(c * CHUNK, CHUNK), :],
            preferred_element_type=jnp.float32,
        )
    return total + jnp.sum(lane_total, axis=1, keepdims=True), acc


def first_kernel(
    q_ref,
    pos_ref,
    wk_ref,
    wv_ref,
    xk_ref,
    xv_ref,
    acc_ref,
    top_ref,
    total_ref,
    score_ref,
    *,
    extra_sinks,
    per_device,
    stride,
):
    rows = q_ref.shape[0]
    scale = 1.0 / math.sqrt(HEAD_DIM)
    q_stack = stacked_queries(q_ref)
    stacked = q_stack.shape[0]
    nt = (((1,), (1,)), ((), ()))
    extra_rows = xk_ref.shape[0]
    extra = (
        lax.dot_general(q_stack, xk_ref[...], nt, preferred_element_type=jnp.float32) * scale
    )
    extra_pos = lax.broadcasted_iota(jnp.int32, (stacked, extra_rows), 0) % rows
    extra_key = lax.broadcasted_iota(jnp.int32, (stacked, extra_rows), 1)
    extra_visible = (extra_key <= extra_pos) | (
        (extra_key >= rows) & (extra_key < rows + extra_sinks)
    )
    extra = jnp.where(extra_visible, extra, -jnp.inf)
    top = jnp.maximum(
        jnp.max(extra, axis=1, keepdims=True),
        window_scores(q_stack, pos_ref, wk_ref, score_ref, rows, per_device, stride, scale),
    )
    e = jnp.exp(extra - top)
    total = jnp.sum(e, axis=1, keepdims=True)
    acc = jnp.dot(e.astype(jnp.bfloat16), xv_ref[...], preferred_element_type=jnp.float32)
    total, acc = window_sums(wv_ref, score_ref, top, total, acc)
    acc_ref[...] = acc
    top_ref[...] = jnp.broadcast_to(top, top_ref.shape)
    total_ref[...] = jnp.broadcast_to(total, total_ref.shape)


def second_kernel(
    q_ref,
    pos_ref,
    wk_ref,
    wv_ref,
    acc_ref,
    top_ref,
    total_ref,
    logits_ref,
    pick0_ref,
    pick1_ref,
    live_ref,
    out_ref,
    score_ref,
    *,
    per_device,
    stride,
):
    rows = q_ref.shape[0]
    scale = 1.0 / math.sqrt(HEAD_DIM)
    q_stack = stacked_queries(q_ref)
    first_top = top_ref[:, 0:1]
    top = jnp.maximum(
        first_top,
        window_scores(q_stack, pos_ref, wk_ref, score_ref, rows, per_device, stride, scale),
    )
    factor = jnp.exp(first_top - top)
    total, acc = window_sums(
        wv_ref, score_ref, top, total_ref[:, 0:1] * factor, acc_ref[...] * factor
    )
    attended = acc / total
    logits = logits_ref[...]
    chosen0 = jnp.sum(jnp.where(pick0_ref[...] != 0, logits, 0.0), axis=0, keepdims=True)
    chosen1 = jnp.sum(jnp.where(pick1_ref[...] != 0, logits, 0.0), axis=0, keepdims=True)
    live = live_ref[...] != 0
    gate_rows = jnp.concatenate(
        [
            jnp.where(live, jax.nn.sigmoid(chosen0 - chosen1), 0.0),
            jnp.where(live, jax.nn.sigmoid(chosen1 - chosen0), 0.0),
            jnp.zeros((logits.shape[0] - PICKS, logits.shape[1]), jnp.float32),
        ],
        axis=0,
    )
    gate_cols = jnp.transpose(gate_rows)
    gate0 = gate_cols[:, 0:1]
    gate1 = gate_cols[:, 1:2]
    out_ref[:, :HEAD_DIM] = (attended[:rows] * gate0).astype(out_ref.dtype)
    out_ref[:, HEAD_DIM:] = (attended[rows:] * gate1).astype(out_ref.dtype)


def attend_first(queries, key_pos, parts, plane_rows, extra, head_count, extra_sinks, per_device):
    rows = queries.shape[0]
    stacked = PICKS * rows
    extra_rows = extra.shape[0]
    first, second = parts
    first_rows = first.shape[0]
    second_rows = second.shape[0]
    first_pos = key_pos[:, :first_rows]
    second_pos = key_pos[:, first_rows:]
    q_spec = pl.BlockSpec((rows, PICKS * HEAD_DIM), lambda h: (0, h))
    state_spec = pl.BlockSpec((None, stacked, HEAD_DIM), lambda h: (h, 0, 0))
    state_shape = jax.ShapeDtypeStruct((head_count, stacked, HEAD_DIM), jnp.float32)

    def key_spec(part_rows):
        return pl.BlockSpec((part_rows, HEAD_DIM), lambda h: (0, h))

    def value_spec(part_rows):
        return pl.BlockSpec((part_rows, HEAD_DIM), lambda h: (0, head_count + h))

    acc, top, total = pl.pallas_call(
        functools.partial(
            first_kernel, extra_sinks=extra_sinks, per_device=per_device, stride=plane_rows[0]
        ),
        grid=(head_count,),
        in_specs=[
            q_spec,
            pl.BlockSpec((1, first_rows), lambda h: (0, 0)),
            key_spec(first_rows),
            value_spec(first_rows),
            key_spec(extra_rows),
            value_spec(extra_rows),
        ],
        out_specs=[state_spec, state_spec, state_spec],
        scratch_shapes=[pltpu.VMEM((stacked, first_rows), jnp.float32)],
        out_shape=[state_shape, state_shape, state_shape],
    )(queries, first_pos, first, first, extra, extra)
    return acc, top, total


def attend_second(queries, key_pos, parts, plane_rows, state, gate_inputs, head_count, per_device):
    rows = queries.shape[0]
    stacked = PICKS * rows
    first, second = parts
    first_rows = first.shape[0]
    second_rows = second.shape[0]
    second_pos = key_pos[:, first_rows:]
    acc, top, total = state
    q_spec = pl.BlockSpec((rows, PICKS * HEAD_DIM), lambda h: (0, h))
    state_spec = pl.BlockSpec((None, stacked, HEAD_DIM), lambda h: (h, 0, 0))

    def key_spec(part_rows):
        return pl.BlockSpec((part_rows, HEAD_DIM), lambda h: (0, h))

    def value_spec(part_rows):
        return pl.BlockSpec((part_rows, HEAD_DIM), lambda h: (0, head_count + h))

    return pl.pallas_call(
        functools.partial(second_kernel, per_device=per_device, stride=plane_rows[1]),
        grid=(head_count,),
        in_specs=[
            q_spec,
            pl.BlockSpec((1, second_rows), lambda h: (0, 0)),
            key_spec(second_rows),
            value_spec(second_rows),
            state_spec,
            state_spec,
            state_spec,
        ]
        + [pl.BlockSpec(value.shape, lambda h: (0, 0)) for value in gate_inputs],
        out_specs=q_spec,
        scratch_shapes=[pltpu.VMEM((stacked, second_rows), jnp.float32)],
        out_shape=jax.ShapeDtypeStruct((rows, head_count * PICKS * HEAD_DIM), jnp.bfloat16),
    )(queries, second_pos, second, second, acc, top, total, *gate_inputs)


def body(queries, suffix_kv, window_kv, sink_kv, lengths, group_ids, hidden_in, router, picks):
    row_count = queries.shape[0]
    head_count = suffix_kv.shape[2] // HEAD_DIM
    partial_value = jnp.dot(hidden_in, router, preferred_element_type=jnp.float32)
    z_count = lax.axis_size("z")
    plane_count = lax.axis_size("ylo") * lax.axis_size("x")
    z_me = lax.axis_index("z")
    plane_me = lax.axis_index("ylo") * lax.axis_size("x") + lax.axis_index("x")
    my_group = group_ids[z_me * plane_count + plane_me]

    width = 2 * head_count * HEAD_DIM
    per_device = window_kv.shape[1]
    local = window_kv.reshape(window_kv.shape[0], per_device, width)
    def shifted(value, shift):
        pairs = [(j, (j + shift) % z_count) for j in range(z_count)]
        return lax.ppermute(value, "z", pairs)

    half = per_device // 2
    up = shifted(local, 1)
    down = shifted(local, z_count - 1)
    far_up = shifted(jnp.concatenate([down, local, up[:, :half]], axis=1), 3)
    far_down = shifted(jnp.concatenate([local, up, down[:, half:]], axis=1), z_count - 3)
    near_pieces = ((0, 0, per_device), (1, 0, per_device), (z_count - 1, 0, per_device))
    far_pieces = (
        (2, 0, per_device),
        (3, 0, per_device),
        (4, 0, half),
        (z_count - 3, 0, per_device),
        (z_count - 2, 0, per_device),
        (4, half, per_device - half),
    )
    part_pieces = (near_pieces, far_pieces)
    part_data = (jnp.concatenate([local, up, down], axis=1), jnp.concatenate([far_up, far_down], axis=1))
    peer_groups = lax.dynamic_slice_in_dim(group_ids, z_me * plane_count, plane_count)
    plane_ids = jnp.arange(plane_count, dtype=jnp.int32)
    parts = []
    positions = []
    for pieces, data in zip(part_pieces, part_data):
        outgoing = jnp.where((peer_groups == 0)[:, None, None], data[None, 0], data[None, 1])
        received = lax.all_to_all(
            outgoing, ("ylo", "x"), split_axis=0, concat_axis=0, tiled=True
        )
        parts.append(received.reshape(plane_count * data.shape[1], width))
        piece_pos = []
        for shift, first, count in pieces:
            z_of = (z_me - shift) % z_count
            rows_of = first + jnp.arange(count, dtype=jnp.int32)
            piece_pos.append(
                (z_of * plane_count + plane_ids[:, None]) * per_device + rows_of[None, :]
            )
        positions.append(jnp.concatenate(piece_pos, axis=1).reshape(-1))

    sink_rows = lax.dynamic_index_in_dim(sink_kv, my_group, 0, keepdims=False)
    sink_count = sink_rows.shape[0]
    extra_rows = 2 * row_count
    extra = jnp.concatenate(
        [
            suffix_kv.reshape(row_count, width),
            sink_rows.reshape(sink_count, width),
            jnp.zeros((extra_rows - row_count - sink_count, width), suffix_kv.dtype),
        ],
        axis=0,
    )
    key_pos = jnp.concatenate(positions).reshape(1, -1)
    plane_rows = tuple(data.shape[1] for data in part_data)
    state = attend_first(queries, key_pos, parts, plane_rows, extra, head_count, sink_count, per_device)
    state, partial_value = lax.optimization_barrier((state, partial_value))
    logits = lax.psum(partial_value, "tp")
    experts = jnp.arange(logits.shape[1], dtype=jnp.int32)
    pick0 = (picks[:, 0][None, :] == experts[:, None]).astype(jnp.int32)
    pick1 = (picks[:, 1][None, :] == experts[:, None]).astype(jnp.int32)
    is_live = (jnp.arange(row_count, dtype=jnp.int32) < lengths[0]).astype(jnp.int32)
    gate_inputs = (jnp.transpose(logits), pick0, pick1, is_live[None, :])
    return attend_second(
        queries, key_pos, parts, plane_rows, state, gate_inputs, head_count, per_device
    )


def solution(mesh):
    plane_ylo, plane_x = 2, 4
    z_count = mesh.shape["req"] // (plane_ylo * plane_x)
    devices = mesh.devices.reshape(z_count, plane_ylo, plane_x, mesh.shape["tp"])
    inner = jax.sharding.Mesh(devices, ("z", "ylo", "x", "tp"))
    req = ("z", "ylo", "x")
    return jax.shard_map(
        body,
        mesh=inner,
        in_specs=(
            P(req, "tp"),
            P(req, None, "tp"),
            P(None, req, None, "tp"),
            P(None, None, None, "tp"),
            P(req),
            P(),
            P(req, "tp"),
            P("tp", None),
            P(req, None),
        ),
        out_specs=P(req, "tp"),
        check_vma=False,
    )
```

```python
import functools
import math

import jax
import jax.numpy as jnp
from jax import lax
from jax.experimental import pallas as pl
from jax.experimental.pallas import tpu as pltpu
from jax.sharding import PartitionSpec as P

HEAD_DIM = 128
PICKS = 2
CHUNK = 512


def stacked_queries(q_ref):
    q = q_ref[...]
    return jnp.concatenate([q[:, :HEAD_DIM], q[:, HEAD_DIM:]], axis=0)


def window_scores(q_stack, pos_ref, wk_ref, score_ref, rows, per_device, stride, scale):
    stacked = q_stack.shape[0]
    query_pos = lax.broadcasted_iota(jnp.int32, (stacked, 1), 0) % rows
    nt = (((1,), (1,)), ((), ()))
    lane_top = jnp.full((stacked, HEAD_DIM), -jnp.inf, jnp.float32)
    for c in range(wk_ref.shape[0] // CHUNK):
        keys = wk_ref[pl.ds(c * CHUNK, CHUNK), :]
        s = lax.dot_general(q_stack, keys, nt, preferred_element_type=jnp.float32) * scale
        if (c * CHUNK) // stride * per_device < rows:
            key_pos = pos_ref[:, pl.ds(c * CHUNK, CHUNK)]
            s = jnp.where(key_pos > query_pos, s, -jnp.inf)
        score_ref[:, pl.ds(c * CHUNK, CHUNK)] = s
        for j in range(CHUNK // HEAD_DIM):
            lane_top = jnp.maximum(lane_top, s[:, j * HEAD_DIM : (j + 1) * HEAD_DIM])
    return jnp.max(lane_top, axis=1, keepdims=True)


def window_sums(wv_ref, score_ref, top, total, acc):
    lane_total = jnp.zeros((top.shape[0], HEAD_DIM), jnp.float32)
    for c in range(wv_ref.shape[0] // CHUNK):
        e = jnp.exp(score_ref[:, pl.ds(c * CHUNK, CHUNK)] - top)
        for j in range(CHUNK // HEAD_DIM):
            lane_total = lane_total + e[:, j * HEAD_DIM : (j + 1) * HEAD_DIM]
        acc = acc + jnp.dot(
            e.astype(jnp.bfloat16),
            wv_ref[pl.ds(c * CHUNK, CHUNK), :],
            preferred_element_type=jnp.float32,
        )
    return total + jnp.sum(lane_total, axis=1, keepdims=True), acc


def first_kernel(
    q_ref,
    pos_ref,
    wk_ref,
    wv_ref,
    xk_ref,
    xv_ref,
    acc_ref,
    top_ref,
    total_ref,
    score_ref,
    *,
    extra_sinks,
    per_device,
    stride,
):
    rows = q_ref.shape[0]
    scale = 1.0 / math.sqrt(HEAD_DIM)
    q_stack = stacked_queries(q_ref)
    stacked = q_stack.shape[0]
    nt = (((1,), (1,)), ((), ()))
    extra_rows = xk_ref.shape[0]
    extra = (
        lax.dot_general(q_stack, xk_ref[...], nt, preferred_element_type=jnp.float32) * scale
    )
    extra_pos = lax.broadcasted_iota(jnp.int32, (stacked, extra_rows), 0) % rows
    extra_key = lax.broadcasted_iota(jnp.int32, (stacked, extra_rows), 1)
    extra_visible = (extra_key <= extra_pos) | (
        (extra_key >= rows) & (extra_key < rows + extra_sinks)
    )
    extra = jnp.where(extra_visible, extra, -jnp.inf)
    top = jnp.maximum(
        jnp.max(extra, axis=1, keepdims=True),
        window_scores(q_stack, pos_ref, wk_ref, score_ref, rows, per_device, stride, scale),
    )
    e = jnp.exp(extra - top)
    total = jnp.sum(e, axis=1, keepdims=True)
    acc = jnp.dot(e.astype(jnp.bfloat16), xv_ref[...], preferred_element_type=jnp.float32)
    total, acc = window_sums(wv_ref, score_ref, top, total, acc)
    acc_ref[...] = acc
    top_ref[...] = jnp.broadcast_to(top, top_ref.shape)
    total_ref[...] = jnp.broadcast_to(total, total_ref.shape)


def second_kernel(
    q_ref,
    pos_ref,
    wk_ref,
    wv_ref,
    acc_ref,
    top_ref,
    total_ref,
    logits_ref,
    pick0_ref,
    pick1_ref,
    live_ref,
    out_ref,
    score_ref,
    *,
    per_device,
    stride,
):
    rows = q_ref.shape[0]
    scale = 1.0 / math.sqrt(HEAD_DIM)
    q_stack = stacked_queries(q_ref)
    query_pos = lax.broadcasted_iota(jnp.int32, (q_stack.shape[0], 1), 0) % rows
    nt = (((1,), (1,)), ((), ()))
    top = top_ref[:, 0:1]
    total = total_ref[:, 0:1]
    acc = acc_ref[...]
    for c in range(wk_ref.shape[0] // CHUNK):
        keys = wk_ref[pl.ds(c * CHUNK, CHUNK), :]
        s = lax.dot_general(q_stack, keys, nt, preferred_element_type=jnp.float32) * scale
        if (c * CHUNK) // stride * per_device < rows:
            key_pos = pos_ref[:, pl.ds(c * CHUNK, CHUNK)]
            s = jnp.where(key_pos > query_pos, s, -jnp.inf)
        new_top = jnp.maximum(top, jnp.max(s, axis=1, keepdims=True))
        factor = jnp.exp(top - new_top)
        e = jnp.exp(s - new_top)
        total = total * factor + jnp.sum(e, axis=1, keepdims=True)
        acc = acc * factor + jnp.dot(
            e.astype(jnp.bfloat16),
            wv_ref[pl.ds(c * CHUNK, CHUNK), :],
            preferred_element_type=jnp.float32,
        )
        top = new_top
    attended = acc / total
    logits = logits_ref[...]
    chosen0 = jnp.sum(jnp.where(pick0_ref[...] != 0, logits, 0.0), axis=0, keepdims=True)
    chosen1 = jnp.sum(jnp.where(pick1_ref[...] != 0, logits, 0.0), axis=0, keepdims=True)
    live = live_ref[...] != 0
    gate_rows = jnp.concatenate(
        [
            jnp.where(live, jax.nn.sigmoid(chosen0 - chosen1), 0.0),
            jnp.where(live, jax.nn.sigmoid(chosen1 - chosen0), 0.0),
            jnp.zeros((logits.shape[0] - PICKS, logits.shape[1]), jnp.float32),
        ],
        axis=0,
    )
    gate_cols = jnp.transpose(gate_rows)
    gate0 = gate_cols[:, 0:1]
    gate1 = gate_cols[:, 1:2]
    out_ref[:, :HEAD_DIM] = (attended[:rows] * gate0).astype(out_ref.dtype)
    out_ref[:, HEAD_DIM:] = (attended[rows:] * gate1).astype(out_ref.dtype)


def attend_first(queries, key_pos, parts, plane_rows, extra, head_count, extra_sinks, per_device):
    rows = queries.shape[0]
    stacked = PICKS * rows
    extra_rows = extra.shape[0]
    first, second = parts
    first_rows = first.shape[0]
    second_rows = second.shape[0]
    first_pos = key_pos[:, :first_rows]
    second_pos = key_pos[:, first_rows:]
    q_spec = pl.BlockSpec((rows, PICKS * HEAD_DIM), lambda h: (0, h))
    state_spec = pl.BlockSpec((None, stacked, HEAD_DIM), lambda h: (h, 0, 0))
    state_shape = jax.ShapeDtypeStruct((head_count, stacked, HEAD_DIM), jnp.float32)

    def key_spec(part_rows):
        return pl.BlockSpec((part_rows, HEAD_DIM), lambda h: (0, h))

    def value_spec(part_rows):
        return pl.BlockSpec((part_rows, HEAD_DIM), lambda h: (0, head_count + h))

    acc, top, total = pl.pallas_call(
        functools.partial(
            first_kernel, extra_sinks=extra_sinks, per_device=per_device, stride=plane_rows[0]
        ),
        grid=(head_count,),
        in_specs=[
            q_spec,
            pl.BlockSpec((1, first_rows), lambda h: (0, 0)),
            key_spec(first_rows),
            value_spec(first_rows),
            key_spec(extra_rows),
            value_spec(extra_rows),
        ],
        out_specs=[state_spec, state_spec, state_spec],
        scratch_shapes=[pltpu.VMEM((stacked, first_rows), jnp.float32)],
        out_shape=[state_shape, state_shape, state_shape],
    )(queries, first_pos, first, first, extra, extra)
    return acc, top, total


def attend_second(queries, key_pos, parts, plane_rows, state, gate_inputs, head_count, per_device):
    rows = queries.shape[0]
    stacked = PICKS * rows
    first, second = parts
    first_rows = first.shape[0]
    second_rows = second.shape[0]
    second_pos = key_pos[:, first_rows:]
    acc, top, total = state
    q_spec = pl.BlockSpec((rows, PICKS * HEAD_DIM), lambda h: (0, h))
    state_spec = pl.BlockSpec((None, stacked, HEAD_DIM), lambda h: (h, 0, 0))

    def key_spec(part_rows):
        return pl.BlockSpec((part_rows, HEAD_DIM), lambda h: (0, h))

    def value_spec(part_rows):
        return pl.BlockSpec((part_rows, HEAD_DIM), lambda h: (0, head_count + h))

    return pl.pallas_call(
        functools.partial(second_kernel, per_device=per_device, stride=plane_rows[1]),
        grid=(head_count,),
        in_specs=[
            q_spec,
            pl.BlockSpec((1, second_rows), lambda h: (0, 0)),
            key_spec(second_rows),
            value_spec(second_rows),
            state_spec,
            state_spec,
            state_spec,
        ]
        + [pl.BlockSpec(value.shape, lambda h: (0, 0)) for value in gate_inputs],
        out_specs=q_spec,
        scratch_shapes=[pltpu.VMEM((stacked, second_rows), jnp.float32)],
        out_shape=jax.ShapeDtypeStruct((rows, head_count * PICKS * HEAD_DIM), jnp.bfloat16),
    )(queries, second_pos, second, second, acc, top, total, *gate_inputs)


def body(queries, suffix_kv, window_kv, sink_kv, lengths, group_ids, hidden_in, router, picks):
    row_count = queries.shape[0]
    head_count = suffix_kv.shape[2] // HEAD_DIM
    partial_value = jnp.dot(hidden_in, router, preferred_element_type=jnp.float32)
    z_count = lax.axis_size("z")
    plane_count = lax.axis_size("ylo") * lax.axis_size("x")
    z_me = lax.axis_index("z")
    plane_me = lax.axis_index("ylo") * lax.axis_size("x") + lax.axis_index("x")
    my_group = group_ids[z_me * plane_count + plane_me]

    width = 2 * head_count * HEAD_DIM
    per_device = window_kv.shape[1]
    local = window_kv.reshape(window_kv.shape[0], per_device, width)
    def shifted(value, shift):
        pairs = [(j, (j + shift) % z_count) for j in range(z_count)]
        return lax.ppermute(value, "z", pairs)

    half = per_device // 2
    up = shifted(local, 1)
    down = shifted(local, z_count - 1)
    far_up = shifted(jnp.concatenate([down, local, up[:, :half]], axis=1), 3)
    far_down = shifted(jnp.concatenate([local, up, down[:, half:]], axis=1), z_count - 3)
    near_pieces = ((0, 0, per_device), (1, 0, per_device), (z_count - 1, 0, per_device))
    far_pieces = (
        (2, 0, per_device),
        (3, 0, per_device),
        (4, 0, half),
        (z_count - 3, 0, per_device),
        (z_count - 2, 0, per_device),
        (4, half, per_device - half),
    )
    part_pieces = (near_pieces, far_pieces)
    part_data = (jnp.concatenate([local, up, down], axis=1), jnp.concatenate([far_up, far_down], axis=1))
    peer_groups = lax.dynamic_slice_in_dim(group_ids, z_me * plane_count, plane_count)
    plane_ids = jnp.arange(plane_count, dtype=jnp.int32)
    parts = []
    positions = []
    for pieces, data in zip(part_pieces, part_data):
        outgoing = jnp.where((peer_groups == 0)[:, None, None], data[None, 0], data[None, 1])
        received = lax.all_to_all(
            outgoing, ("ylo", "x"), split_axis=0, concat_axis=0, tiled=True
        )
        parts.append(received.reshape(plane_count * data.shape[1], width))
        piece_pos = []
        for shift, first, count in pieces:
            z_of = (z_me - shift) % z_count
            rows_of = first + jnp.arange(count, dtype=jnp.int32)
            piece_pos.append(
                (z_of * plane_count + plane_ids[:, None]) * per_device + rows_of[None, :]
            )
        positions.append(jnp.concatenate(piece_pos, axis=1).reshape(-1))

    sink_rows = lax.dynamic_index_in_dim(sink_kv, my_group, 0, keepdims=False)
    sink_count = sink_rows.shape[0]
    extra_rows = 2 * row_count
    extra = jnp.concatenate(
        [
            suffix_kv.reshape(row_count, width),
            sink_rows.reshape(sink_count, width),
            jnp.zeros((extra_rows - row_count - sink_count, width), suffix_kv.dtype),
        ],
        axis=0,
    )
    key_pos = jnp.concatenate(positions).reshape(1, -1)
    plane_rows = tuple(data.shape[1] for data in part_data)
    state = attend_first(queries, key_pos, parts, plane_rows, extra, head_count, sink_count, per_device)
    state, partial_value = lax.optimization_barrier((state, partial_value))
    logits = lax.psum(partial_value, "tp")
    experts = jnp.arange(logits.shape[1], dtype=jnp.int32)
    pick0 = (picks[:, 0][None, :] == experts[:, None]).astype(jnp.int32)
    pick1 = (picks[:, 1][None, :] == experts[:, None]).astype(jnp.int32)
    is_live = (jnp.arange(row_count, dtype=jnp.int32) < lengths[0]).astype(jnp.int32)
    gate_inputs = (jnp.transpose(logits), pick0, pick1, is_live[None, :])
    return attend_second(
        queries, key_pos, parts, plane_rows, state, gate_inputs, head_count, per_device
    )


def solution(mesh):
    plane_ylo, plane_x = 2, 4
    z_count = mesh.shape["req"] // (plane_ylo * plane_x)
    devices = mesh.devices.reshape(z_count, plane_ylo, plane_x, mesh.shape["tp"])
    inner = jax.sharding.Mesh(devices, ("z", "ylo", "x", "tp"))
    req = ("z", "ylo", "x")
    return jax.shard_map(
        body,
        mesh=inner,
        in_specs=(
            P(req, "tp"),
            P(req, None, "tp"),
            P(None, req, None, "tp"),
            P(None, None, None, "tp"),
            P(req),
            P(),
            P(req, "tp"),
            P("tp", None),
            P(req, None),
        ),
        out_specs=P(req, "tp"),
        check_vma=False,
    )
```

```python
import functools
import math

import jax
import jax.numpy as jnp
from jax import lax
from jax.experimental import pallas as pl
from jax.experimental.pallas import tpu as pltpu
from jax.sharding import PartitionSpec as P

HEAD_DIM = 128
PICKS = 2
CHUNK = 256


def stacked_queries(q_ref):
    q = q_ref[...]
    return jnp.concatenate([q[:, :HEAD_DIM], q[:, HEAD_DIM:]], axis=0)


def window_scores(q_stack, pos_ref, wk_ref, score_ref, rows, per_device, stride, scale):
    stacked = q_stack.shape[0]
    query_pos = lax.broadcasted_iota(jnp.int32, (stacked, 1), 0) % rows
    nt = (((1,), (1,)), ((), ()))
    lane_top = jnp.full((stacked, HEAD_DIM), -jnp.inf, jnp.float32)
    for c in range(wk_ref.shape[0] // CHUNK):
        keys = wk_ref[pl.ds(c * CHUNK, CHUNK), :]
        s = lax.dot_general(q_stack, keys, nt, preferred_element_type=jnp.float32) * scale
        if (c * CHUNK) // stride * per_device < rows:
            key_pos = pos_ref[:, pl.ds(c * CHUNK, CHUNK)]
            s = jnp.where(key_pos > query_pos, s, -jnp.inf)
        score_ref[:, pl.ds(c * CHUNK, CHUNK)] = s
        for j in range(CHUNK // HEAD_DIM):
            lane_top = jnp.maximum(lane_top, s[:, j * HEAD_DIM : (j + 1) * HEAD_DIM])
    return jnp.max(lane_top, axis=1, keepdims=True)


def window_sums(wv_ref, score_ref, top, total, acc):
    lane_total = jnp.zeros((top.shape[0], HEAD_DIM), jnp.float32)
    for c in range(wv_ref.shape[0] // CHUNK):
        e = jnp.exp(score_ref[:, pl.ds(c * CHUNK, CHUNK)] - top)
        for j in range(CHUNK // HEAD_DIM):
            lane_total = lane_total + e[:, j * HEAD_DIM : (j + 1) * HEAD_DIM]
        acc = acc + jnp.dot(
            e.astype(jnp.bfloat16),
            wv_ref[pl.ds(c * CHUNK, CHUNK), :],
            preferred_element_type=jnp.float32,
        )
    return total + jnp.sum(lane_total, axis=1, keepdims=True), acc


def first_kernel(
    q_ref,
    pos_ref,
    wk_ref,
    wv_ref,
    xk_ref,
    xv_ref,
    acc_ref,
    top_ref,
    total_ref,
    score_ref,
    *,
    extra_sinks,
    per_device,
    stride,
):
    rows = q_ref.shape[0]
    scale = 1.0 / math.sqrt(HEAD_DIM)
    q_stack = stacked_queries(q_ref)
    stacked = q_stack.shape[0]
    nt = (((1,), (1,)), ((), ()))
    extra_rows = xk_ref.shape[0]
    extra = (
        lax.dot_general(q_stack, xk_ref[...], nt, preferred_element_type=jnp.float32) * scale
    )
    extra_pos = lax.broadcasted_iota(jnp.int32, (stacked, extra_rows), 0) % rows
    extra_key = lax.broadcasted_iota(jnp.int32, (stacked, extra_rows), 1)
    extra_visible = (extra_key <= extra_pos) | (
        (extra_key >= rows) & (extra_key < rows + extra_sinks)
    )
    extra = jnp.where(extra_visible, extra, -jnp.inf)
    top = jnp.maximum(
        jnp.max(extra, axis=1, keepdims=True),
        window_scores(q_stack, pos_ref, wk_ref, score_ref, rows, per_device, stride, scale),
    )
    e = jnp.exp(extra - top)
    total = jnp.sum(e, axis=1, keepdims=True)
    acc = jnp.dot(e.astype(jnp.bfloat16), xv_ref[...], preferred_element_type=jnp.float32)
    total, acc = window_sums(wv_ref, score_ref, top, total, acc)
    acc_ref[...] = acc
    top_ref[...] = jnp.broadcast_to(top, top_ref.shape)
    total_ref[...] = jnp.broadcast_to(total, total_ref.shape)


def second_kernel(
    q_ref,
    pos_ref,
    wk_ref,
    wv_ref,
    acc_ref,
    top_ref,
    total_ref,
    logits_ref,
    pick0_ref,
    pick1_ref,
    live_ref,
    out_ref,
    score_ref,
    *,
    per_device,
    stride,
):
    rows = q_ref.shape[0]
    scale = 1.0 / math.sqrt(HEAD_DIM)
    q_stack = stacked_queries(q_ref)
    first_top = top_ref[:, 0:1]
    top = jnp.maximum(
        first_top,
        window_scores(q_stack, pos_ref, wk_ref, score_ref, rows, per_device, stride, scale),
    )
    factor = jnp.exp(first_top - top)
    total, acc = window_sums(
        wv_ref, score_ref, top, total_ref[:, 0:1] * factor, acc_ref[...] * factor
    )
    attended = acc / total
    logits = logits_ref[...]
    chosen0 = jnp.sum(jnp.where(pick0_ref[...] != 0, logits, 0.0), axis=0, keepdims=True)
    chosen1 = jnp.sum(jnp.where(pick1_ref[...] != 0, logits, 0.0), axis=0, keepdims=True)
    live = live_ref[...] != 0
    gate_rows = jnp.concatenate(
        [
            jnp.where(live, jax.nn.sigmoid(chosen0 - chosen1), 0.0),
            jnp.where(live, jax.nn.sigmoid(chosen1 - chosen0), 0.0),
            jnp.zeros((logits.shape[0] - PICKS, logits.shape[1]), jnp.float32),
        ],
        axis=0,
    )
    gate_cols = jnp.transpose(gate_rows)
    gate0 = gate_cols[:, 0:1]
    gate1 = gate_cols[:, 1:2]
    out_ref[:, :HEAD_DIM] = (attended[:rows] * gate0).astype(out_ref.dtype)
    out_ref[:, HEAD_DIM:] = (attended[rows:] * gate1).astype(out_ref.dtype)


def attend_first(queries, key_pos, parts, plane_rows, extra, head_count, extra_sinks, per_device):
    rows = queries.shape[0]
    stacked = PICKS * rows
    extra_rows = extra.shape[0]
    first, second = parts
    first_rows = first.shape[0]
    second_rows = second.shape[0]
    first_pos = key_pos[:, :first_rows]
    second_pos = key_pos[:, first_rows:]
    q_spec = pl.BlockSpec((rows, PICKS * HEAD_DIM), lambda h: (0, h))
    state_spec = pl.BlockSpec((None, stacked, HEAD_DIM), lambda h: (h, 0, 0))
    state_shape = jax.ShapeDtypeStruct((head_count, stacked, HEAD_DIM), jnp.float32)

    def key_spec(part_rows):
        return pl.BlockSpec((part_rows, HEAD_DIM), lambda h: (0, h))

    def value_spec(part_rows):
        return pl.BlockSpec((part_rows, HEAD_DIM), lambda h: (0, head_count + h))

    acc, top, total = pl.pallas_call(
        functools.partial(
            first_kernel, extra_sinks=extra_sinks, per_device=per_device, stride=plane_rows[0]
        ),
        grid=(head_count,),
        in_specs=[
            q_spec,
            pl.BlockSpec((1, first_rows), lambda h: (0, 0)),
            key_spec(first_rows),
            value_spec(first_rows),
            key_spec(extra_rows),
            value_spec(extra_rows),
        ],
        out_specs=[state_spec, state_spec, state_spec],
        scratch_shapes=[pltpu.VMEM((stacked, first_rows), jnp.float32)],
        out_shape=[state_shape, state_shape, state_shape],
    )(queries, first_pos, first, first, extra, extra)
    return acc, top, total


def attend_second(queries, key_pos, parts, plane_rows, state, gate_inputs, head_count, per_device):
    rows = queries.shape[0]
    stacked = PICKS * rows
    first, second = parts
    first_rows = first.shape[0]
    second_rows = second.shape[0]
    second_pos = key_pos[:, first_rows:]
    acc, top, total = state
    q_spec = pl.BlockSpec((rows, PICKS * HEAD_DIM), lambda h: (0, h))
    state_spec = pl.BlockSpec((None, stacked, HEAD_DIM), lambda h: (h, 0, 0))

    def key_spec(part_rows):
        return pl.BlockSpec((part_rows, HEAD_DIM), lambda h: (0, h))

    def value_spec(part_rows):
        return pl.BlockSpec((part_rows, HEAD_DIM), lambda h: (0, head_count + h))

    return pl.pallas_call(
        functools.partial(second_kernel, per_device=per_device, stride=plane_rows[1]),
        grid=(head_count,),
        in_specs=[
            q_spec,
            pl.BlockSpec((1, second_rows), lambda h: (0, 0)),
            key_spec(second_rows),
            value_spec(second_rows),
            state_spec,
            state_spec,
            state_spec,
        ]
        + [pl.BlockSpec(value.shape, lambda h: (0, 0)) for value in gate_inputs],
        out_specs=q_spec,
        scratch_shapes=[pltpu.VMEM((stacked, second_rows), jnp.float32)],
        out_shape=jax.ShapeDtypeStruct((rows, head_count * PICKS * HEAD_DIM), jnp.bfloat16),
    )(queries, second_pos, second, second, acc, top, total, *gate_inputs)


def body(queries, suffix_kv, window_kv, sink_kv, lengths, group_ids, hidden_in, router, picks):
    row_count = queries.shape[0]
    head_count = suffix_kv.shape[2] // HEAD_DIM
    partial_value = jnp.dot(hidden_in, router, preferred_element_type=jnp.float32)
    z_count = lax.axis_size("z")
    plane_count = lax.axis_size("ylo") * lax.axis_size("x")
    z_me = lax.axis_index("z")
    plane_me = lax.axis_index("ylo") * lax.axis_size("x") + lax.axis_index("x")
    my_group = group_ids[z_me * plane_count + plane_me]

    width = 2 * head_count * HEAD_DIM
    per_device = window_kv.shape[1]
    local = window_kv.reshape(window_kv.shape[0], per_device, width)
    def shifted(value, shift):
        pairs = [(j, (j + shift) % z_count) for j in range(z_count)]
        return lax.ppermute(value, "z", pairs)

    half = per_device // 2
    up = shifted(local, 1)
    down = shifted(local, z_count - 1)
    far_up = shifted(jnp.concatenate([down, local, up[:, :half]], axis=1), 3)
    far_down = shifted(jnp.concatenate([local, up, down[:, half:]], axis=1), z_count - 3)
    near_pieces = ((0, 0, per_device), (1, 0, per_device), (z_count - 1, 0, per_device))
    far_pieces = (
        (2, 0, per_device),
        (3, 0, per_device),
        (4, 0, half),
        (z_count - 3, 0, per_device),
        (z_count - 2, 0, per_device),
        (4, half, per_device - half),
    )
    part_pieces = (near_pieces, far_pieces)
    part_data = (jnp.concatenate([local, up, down], axis=1), jnp.concatenate([far_up, far_down], axis=1))
    peer_groups = lax.dynamic_slice_in_dim(group_ids, z_me * plane_count, plane_count)
    plane_ids = jnp.arange(plane_count, dtype=jnp.int32)
    parts = []
    positions = []
    for pieces, data in zip(part_pieces, part_data):
        outgoing = jnp.where((peer_groups == 0)[:, None, None], data[None, 0], data[None, 1])
        received = lax.all_to_all(
            outgoing, ("ylo", "x"), split_axis=0, concat_axis=0, tiled=True
        )
        parts.append(received.reshape(plane_count * data.shape[1], width))
        piece_pos = []
        for shift, first, count in pieces:
            z_of = (z_me - shift) % z_count
            rows_of = first + jnp.arange(count, dtype=jnp.int32)
            piece_pos.append(
                (z_of * plane_count + plane_ids[:, None]) * per_device + rows_of[None, :]
            )
        positions.append(jnp.concatenate(piece_pos, axis=1).reshape(-1))

    sink_rows = lax.dynamic_index_in_dim(sink_kv, my_group, 0, keepdims=False)
    sink_count = sink_rows.shape[0]
    extra_rows = 2 * row_count
    extra = jnp.concatenate(
        [
            suffix_kv.reshape(row_count, width),
            sink_rows.reshape(sink_count, width),
            jnp.zeros((extra_rows - row_count - sink_count, width), suffix_kv.dtype),
        ],
        axis=0,
    )
    key_pos = jnp.concatenate(positions).reshape(1, -1)
    plane_rows = tuple(data.shape[1] for data in part_data)
    state = attend_first(queries, key_pos, parts, plane_rows, extra, head_count, sink_count, per_device)
    state, partial_value = lax.optimization_barrier((state, partial_value))
    logits = lax.psum(partial_value, "tp")
    experts = jnp.arange(logits.shape[1], dtype=jnp.int32)
    pick0 = (picks[:, 0][None, :] == experts[:, None]).astype(jnp.int32)
    pick1 = (picks[:, 1][None, :] == experts[:, None]).astype(jnp.int32)
    is_live = (jnp.arange(row_count, dtype=jnp.int32) < lengths[0]).astype(jnp.int32)
    gate_inputs = (jnp.transpose(logits), pick0, pick1, is_live[None, :])
    return attend_second(
        queries, key_pos, parts, plane_rows, state, gate_inputs, head_count, per_device
    )


def solution(mesh):
    plane_ylo, plane_x = 2, 4
    z_count = mesh.shape["req"] // (plane_ylo * plane_x)
    devices = mesh.devices.reshape(z_count, plane_ylo, plane_x, mesh.shape["tp"])
    inner = jax.sharding.Mesh(devices, ("z", "ylo", "x", "tp"))
    req = ("z", "ylo", "x")
    return jax.shard_map(
        body,
        mesh=inner,
        in_specs=(
            P(req, "tp"),
            P(req, None, "tp"),
            P(None, req, None, "tp"),
            P(None, None, None, "tp"),
            P(req),
            P(),
            P(req, "tp"),
            P("tp", None),
            P(req, None),
        ),
        out_specs=P(req, "tp"),
        check_vma=False,
    )
```
